512 devices in a mesh: layer: 4 (over y), tx: 8 (over x, core), ty: 16 (over z).
Axes of the slice: x: 4, y: 4, z: 16, core: 2. Of those that a mesh axis runs over, the one named last changes fastest.
Arguments:
- shunt_conductance: float32 [4, 256, 2048], P('layer', 'tx', 'ty'), may hold values from 0.02 to 2
- agg_map: int32 [4, 256, 2048], P('layer', 'tx', 'ty'), may hold values from 0 to 127, as said below
- slot_current: float32 [4, 8, 16, 128, 128], P('layer', 'tx', 'ty'), may hold values from -12 to 12
- slot_node: int32 [4, 8, 16, 128, 128], P('layer', 'tx', 'ty'), may hold values from 0 to 4095
- slot_count: int32 [4, 8, 16, 128], P('layer', 'tx', 'ty'), may hold values from 16 to 128, as said below
Outputs:
- voltage_drop: float32 [4, 256, 2048], P('layer', 'tx', 'ty')
- residual: float32 [4, 256, 2048], P('layer', 'tx', 'ty')
The draws below stay inside these ranges and needn't reach their ends.
Inputs may be any that keep to these rules, and one draw needn't show every extreme that they name: `slot_count`: live slots in each block from one source tile to one destination tile, at least 16; slots past them are padding, and at least one block is full. `agg_map`: coarse cell numbered row-major over the 8 x 16 coarse cells of the node's own die tile.
All inputs are finite; a program needn't handle non-finite values.
Results may differ from the reference program's by a relative error of at most 0.0003.
Values sent between devices are 32-bit elements; how exact they have to be, the bound alone decides.
No kernel may reach another device: no remote copies, remote signals or barrier semaphores. Data moves between devices by JAX's collectives and lax.ppermute only.
A program may use at most 64 MiB of HBM per device.

```python
import math
import jax
import jax.numpy as jnp
from jax import lax

CX = 32
CY = 128
CGX = 8
CGY = 16
CAP = 128
ITERS = 3
SWEEPS = 3
LAYERS = 4
NX = 256
NY = 2048
TILES = 128
N_TX = 8
N_TY = 16


def draw_agg_map(key, part):
    shape = (LAYERS, NX, NY)
    block_rows = CX // CGX
    block_cols = CY // CGY
    reach_rows = max(1, block_rows // 4)
    reach_cols = max(1, block_cols // 4)
    first_key = jax.random.fold_in(key, 11)
    second_key = jax.random.fold_in(key, 12)
    shift_rows = jax.random.randint(first_key, shape, -reach_rows, reach_rows + 1)
    shift_cols = jax.random.randint(second_key, shape, -reach_cols, reach_cols + 1)
    local_rows = lax.broadcasted_iota(jnp.int32, shape, 1) % CX
    local_cols = lax.broadcasted_iota(jnp.int32, shape, 2) % CY
    coarse_row = jnp.clip((local_rows + shift_rows) // block_rows, 0, CGX - 1)
    coarse_col = jnp.clip((local_cols + shift_cols) // block_cols, 0, CGY - 1)
    return (coarse_row * CGY + coarse_col).astype(jnp.int32)


def draw_slot_count(key, part):
    shape = (LAYERS, NX // CX, NY // CY, TILES)
    first_key = jax.random.fold_in(key, 21)
    second_key = jax.random.fold_in(key, 22)
    heat = jax.random.randint(first_key, (TILES,), 1, 5)
    base = jax.random.randint(second_key, shape, CAP // 8, CAP // 4 + 1)
    counts = jnp.minimum(CAP, base * heat[None, None, None, :])
    return counts.at[0, 0, 0, 0].set(CAP).astype(jnp.int32)


def with_ends(drawn, own_key, low, high):
    longest = drawn.shape.index(max(drawn.shape))
    spots = []
    for shift in (0, 1):
        where = [jax.random.randint(jax.random.fold_in(own_key, axis), (), 0, length) for axis, length in enumerate(drawn.shape)]
        where[longest] = (where[longest] + shift) % drawn.shape[longest]
        spots.append(tuple(where))
    return drawn.at[spots[0]].set(low).at[spots[1]].set(high)


def block_levels(rng, dims, shards, smallest, top_value):
    gain = 1.0
    for position, shards_of in shards:
        steps = jax.random.uniform(jax.random.fold_in(jax.random.fold_in(rng, 6), position), (shards_of,), jnp.float32, smallest / len(shards), top_value / len(shards))
        gain = gain * jnp.repeat(jnp.exp(steps), dims[position] // shards_of).reshape((-1,) + (1,) * (len(dims) - 1 - position))
    return gain


def bell_draw(key, extent, deviation, most, shards=(), held_as=jnp.bfloat16):
    drawn = deviation * jax.random.normal(key, extent, jnp.float32)
    if shards:
        drawn = drawn * block_levels(key, extent, shards, -0.22, 0.18)
    return jnp.clip(drawn, -most, most).astype(held_as)


def setup_inputs(seed: int = 0) -> dict:
    streams_of = jax.random.split(jax.random.key(seed), 6)
    return {
        "shunt_conductance": jnp.clip(jnp.exp(math.log(2.0) - 4.6051702 * jax.random.uniform(streams_of[0], (LAYERS, NX, NY), jnp.float32) ** block_levels(streams_of[0], (LAYERS, NX, NY), ((0, 4), (1, 8), (2, 16)), -0.2, 0.2)), 0.02, 2.0),
        "agg_map": draw_agg_map(jax.random.fold_in(streams_of[5], 71), 0),
        "slot_current": bell_draw(streams_of[2], (LAYERS, N_TX, N_TY, TILES, CAP), 3.0, 12.0, ((0, 4), (1, 8), (2, 16)), jnp.float32),
        "slot_node": with_ends(jax.random.randint(streams_of[3], (LAYERS, N_TX, N_TY, TILES, CAP), 0, CX * CY), jax.random.fold_in(streams_of[3], 1), 0, (CX * CY) - 1).astype(jnp.int32),
        "slot_count": draw_slot_count(jax.random.fold_in(streams_of[5], 71), 0),
    }


VIA_CONDUCTANCE = 0.5
COARSE_EDGE = 8.0
RELAXATION = 0.6


def operate(source_field, diagonal):
    padded = jnp.pad(source_field, 1)
    lateral = padded[1:-1, 2:, 1:-1] + padded[1:-1, :-2, 1:-1] + padded[1:-1, 1:-1, 2:] + padded[1:-1, 1:-1, :-2]
    vertical = padded[2:, 1:-1, 1:-1] + padded[:-2, 1:-1, 1:-1]
    return diagonal * source_field - lateral - VIA_CONDUCTANCE * vertical


def coarse_sweep(potential, coarse_rhs, coarse_diag, padded):
    beside = padded[..., 2:, 1:-1] + padded[..., :-2, 1:-1] + padded[..., 1:-1, 2:] + padded[..., 1:-1, :-2]
    return potential + RELAXATION * (coarse_rhs - (coarse_diag * potential - COARSE_EDGE * beside)) / coarse_diag


def reference(shunt_conductance, agg_map, slot_current, slot_node, slot_count):
    shape = (LAYERS, NX, NY)
    layer_index = lax.broadcasted_iota(jnp.int32, shape, 0)
    row_index = lax.broadcasted_iota(jnp.int32, shape, 1)
    col_index = lax.broadcasted_iota(jnp.int32, shape, 2)
    coarse_rows = N_TX * CGX
    coarse_cols = N_TY * CGY
    grid_row = (row_index // CX) * CGX + agg_map // CGY
    grid_col = (col_index // CY) * CGY + agg_map % CGY
    coarse_ids = ((layer_index * coarse_rows + grid_row) * coarse_cols + grid_col).reshape(-1).astype(jnp.int32)
    coarse_total = LAYERS * coarse_rows * coarse_cols

    def restrict(source_field):
        summed = jax.ops.segment_sum(source_field.reshape(-1), coarse_ids, coarse_total)
        return summed.reshape(LAYERS, coarse_rows, coarse_cols)

    diagonal = shunt_conductance + (4.0 + 2.0 * VIA_CONDUCTANCE)
    coarse_diag = 4.0 * COARSE_EDGE + restrict(shunt_conductance + 2.0 * VIA_CONDUCTANCE)

    def precondition(residual):
        coarse_rhs = restrict(residual)
        potential = RELAXATION * coarse_rhs / coarse_diag
        for sweep_turn in range(SWEEPS - 1):
            padded = jnp.pad(potential, ((0, 0), (1, 1), (1, 1)))
            potential = coarse_sweep(potential, coarse_rhs, coarse_diag, padded)
        return residual / diagonal + potential.reshape(-1)[coarse_ids].reshape(shape)

    slot_shape = slot_current.shape
    live_mask = lax.broadcasted_iota(jnp.int32, slot_shape, 4) < slot_count[..., None]
    currents = jnp.where(live_mask, slot_current, jnp.zeros_like(slot_current))
    slot_layer = lax.broadcasted_iota(jnp.int32, slot_shape, 0)
    dest_tile = lax.broadcasted_iota(jnp.int32, slot_shape, 3)
    dest_row = (dest_tile // N_TY) * CX + slot_node // CY
    dest_col = (dest_tile % N_TY) * CY + slot_node % CY
    node_ids = ((slot_layer * NX + dest_row) * NY + dest_col).reshape(-1).astype(jnp.int32)
    sources = jax.ops.segment_sum(currents.reshape(-1), node_ids, LAYERS * NX * NY).reshape(shape)

    voltage = jnp.zeros_like(sources)
    residual = sources
    smoothed = precondition(residual)
    direction = smoothed
    curv_now = jnp.sum(residual * smoothed)
    for iteration in range(ITERS):
        image = operate(direction, diagonal)
        step_size = curv_now / jnp.sum(direction * image)
        voltage = voltage + step_size * direction
        residual = residual - step_size * image
        smoothed = precondition(residual)
        curv_next = jnp.sum(residual * smoothed)
        direction = smoothed + (curv_next / curv_now) * direction
        curv_now = curv_next
    return voltage, residual
```

```python
import jax
import jax.numpy as jnp
from jax import lax
from jax.sharding import PartitionSpec as P

CGX = 8
CGY = 16
ITERS = 3
SWEEPS = 3


VIA_CONDUCTANCE = 0.5
COARSE_EDGE = 8.0
RELAXATION = 0.6


def total(vector):
    for axis in ("ty", "tx", "layer"):
        vector = lax.psum(vector, axis)
    return vector


def shift_from(block, axis, offset):
    count = lax.axis_size(axis)
    pairs = [(i + offset, i) for i in range(count) if 0 <= i + offset < count]
    return lax.ppermute(block, axis, pairs)


def shift_from_2d(block, offset_x, offset_y):
    count_x = lax.axis_size("tx")
    count_y = lax.axis_size("ty")
    pairs = []
    for i in range(count_x):
        for j in range(count_y):
            si, sj = i + offset_x, j + offset_y
            if 0 <= si < count_x and 0 <= sj < count_y:
                pairs.append((si * count_y + sj, i * count_y + j))
    return lax.ppermute(block, ("tx", "ty"), pairs)


def coarse_ext(field):
    north = shift_from(field[-2:, :], "tx", -1)
    south = shift_from(field[:2, :], "tx", 1)
    west = shift_from(field[:, -2:], "ty", -1)
    east = shift_from(field[:, :2], "ty", 1)
    north_west = shift_from_2d(field[-2:, -2:], -1, -1)
    north_east = shift_from_2d(field[-2:, :2], -1, 1)
    south_west = shift_from_2d(field[:2, -2:], 1, -1)
    south_east = shift_from_2d(field[:2, :2], 1, 1)
    top = jnp.concatenate([north_west, north, north_east], axis=1)
    middle = jnp.concatenate([west, field, east], axis=1)
    bottom = jnp.concatenate([south_west, south, south_east], axis=1)
    return jnp.concatenate([top, middle, bottom], axis=0)


def operate(source_field, diagonal):
    above = shift_from(source_field, "layer", 1)
    below = shift_from(source_field, "layer", -1)
    north = shift_from(source_field[:, -1:, :], "tx", -1)
    south = shift_from(source_field[:, :1, :], "tx", 1)
    west = shift_from(source_field[:, :, -1:], "ty", -1)
    east = shift_from(source_field[:, :, :1], "ty", 1)
    lateral = (
        jnp.concatenate([source_field[:, 1:, :], south], axis=1)
        + jnp.concatenate([north, source_field[:, :-1, :]], axis=1)
        + jnp.concatenate([source_field[:, :, 1:], east], axis=2)
        + jnp.concatenate([west, source_field[:, :, :-1]], axis=2)
    )
    vertical = above + below
    return diagonal * source_field - lateral - VIA_CONDUCTANCE * vertical


def coarse_sweep(potential, coarse_rhs, coarse_diag, padded):
    beside = (
        padded[..., 2:, 1:-1]
        + padded[..., :-2, 1:-1]
        + padded[..., 1:-1, 2:]
        + padded[..., 1:-1, :-2]
    )
    return (
        potential
        + RELAXATION * (coarse_rhs - (coarse_diag * potential - COARSE_EDGE * beside)) / coarse_diag
    )


def restrict(source_field, gather):
    flat = source_field.reshape(1, -1)
    summed = jnp.dot(
        flat, gather, precision=lax.Precision.HIGHEST, preferred_element_type=jnp.float32
    )
    return summed.reshape(CGX, CGY)


def prolong(potential, gather, shape):
    spread = jnp.dot(
        gather,
        potential.reshape(-1),
        precision=lax.Precision.HIGHEST,
        preferred_element_type=jnp.float32,
    )
    return spread.reshape(shape)


def precondition(residual, diagonal, gather, diag_ext, inside_ext):
    coarse_rhs = coarse_ext(restrict(residual, gather))
    potential = jnp.where(inside_ext, RELAXATION * coarse_rhs / diag_ext, 0.0)
    for sweep_turn in range(SWEEPS - 1):
        potential = coarse_sweep(
            potential[1:-1, 1:-1], coarse_rhs[1:-1, 1:-1], diag_ext[1:-1, 1:-1], potential
        )
        coarse_rhs = coarse_rhs[1:-1, 1:-1]
        diag_ext = diag_ext[1:-1, 1:-1]
        inside_ext = inside_ext[1:-1, 1:-1]
        potential = jnp.where(inside_ext, potential, 0.0)
    return residual / diagonal + prolong(potential, gather, residual.shape)


def body(shunt_conductance, agg_map, slot_current, slot_node, slot_count):
    height = shunt_conductance.shape[1]
    breadth = shunt_conductance.shape[2]
    tile_count = slot_count.shape[3]
    capacity = slot_current.shape[4]
    live_mask = lax.broadcasted_iota(jnp.int32, slot_current.shape, 4) < slot_count[..., None]
    currents = jnp.where(live_mask, slot_current, jnp.zeros_like(slot_current))
    targets = slot_node.astype(jnp.float32)
    packed = jnp.stack(
        [currents.reshape(tile_count, capacity), targets.reshape(tile_count, capacity)], axis=1
    )
    arrived = lax.all_to_all(packed, ("tx", "ty"), split_axis=0, concat_axis=0, tiled=True)
    arrived_current = arrived[:, 0, :].reshape(-1)
    node_ids = arrived[:, 1, :].reshape(-1).astype(jnp.int32)
    row_hit = (
        (node_ids // breadth)[:, None] == lax.broadcasted_iota(jnp.int32, (1, height), 1)
    )
    col_hit = (
        (node_ids % breadth)[:, None] == lax.broadcasted_iota(jnp.int32, (1, breadth), 1)
    ).astype(jnp.float32)
    weighted_rows = jnp.where(row_hit, arrived_current[:, None], 0.0)
    sources = lax.dot_general(
        weighted_rows,
        col_hit,
        (((0,), (0,)), ((), ())),
        precision=lax.Precision.HIGHEST,
        preferred_element_type=jnp.float32,
    ).reshape(1, height, breadth)

    gather = (
        agg_map.reshape(-1)[:, None] == lax.broadcasted_iota(jnp.int32, (1, CGX * CGY), 1)
    ).astype(jnp.float32)
    diagonal = shunt_conductance + (4.0 + 2.0 * VIA_CONDUCTANCE)
    coarse_diag = 4.0 * COARSE_EDGE + restrict(shunt_conductance + 2.0 * VIA_CONDUCTANCE, gather)
    row_of = lax.axis_index("tx") * CGX - 2 + lax.broadcasted_iota(jnp.int32, (CGX + 4, CGY + 4), 0)
    col_of = lax.axis_index("ty") * CGY - 2 + lax.broadcasted_iota(jnp.int32, (CGX + 4, CGY + 4), 1)
    inside_ext = (
        (row_of >= 0)
        & (row_of < lax.axis_size("tx") * CGX)
        & (col_of >= 0)
        & (col_of < lax.axis_size("ty") * CGY)
    )
    diag_ext = jnp.where(inside_ext, coarse_ext(coarse_diag), 1.0)

    voltage = jnp.zeros_like(sources)
    residual = sources
    smoothed = precondition(residual, diagonal, gather, diag_ext, inside_ext)
    direction = smoothed
    image = operate(direction, diagonal)
    sums = total(jnp.stack([jnp.sum(residual * smoothed), jnp.sum(direction * image)]))
    curv_now = sums[0]
    energy = sums[1]
    for iteration in range(ITERS):
        step_size = curv_now / energy
        voltage = voltage + step_size * direction
        residual = residual - step_size * image
        if iteration + 1 < ITERS:
            smoothed = precondition(residual, diagonal, gather, diag_ext, inside_ext)
            smoothed_image = operate(smoothed, diagonal)
            sums = total(
                jnp.stack(
                    [
                        jnp.sum(residual * smoothed),
                        jnp.sum(smoothed * smoothed_image),
                        jnp.sum(smoothed * image),
                        jnp.sum(direction * smoothed_image),
                    ]
                )
            )
            curv_next = sums[0]
            ratio = curv_next / curv_now
            direction = smoothed + ratio * direction
            image = smoothed_image + ratio * image
            energy = sums[1] + ratio * (sums[2] + sums[3]) + ratio * ratio * energy
            curv_now = curv_next
    return (voltage, residual)


def solution(mesh):
    in_specs = (
        P("layer", "tx", "ty"),
        P("layer", "tx", "ty"),
        P("layer", "tx", "ty", None, None),
        P("layer", "tx", "ty", None, None),
        P("layer", "tx", "ty", None),
    )
    out_specs = (P("layer", "tx", "ty"), P("layer", "tx", "ty"))
    return jax.shard_map(body, mesh=mesh, in_specs=in_specs, out_specs=out_specs, check_vma=False)
```

```python
import jax
import jax.numpy as jnp
from jax import lax
from jax.sharding import PartitionSpec as P

CGX = 8
CGY = 16
ITERS = 3
SWEEPS = 3


VIA_CONDUCTANCE = 0.5
COARSE_EDGE = 8.0
RELAXATION = 0.6


def total(vector):
    for axis in ("ty", "tx", "layer"):
        vector = lax.psum(vector, axis)
    return vector


def shift_from(block, axis, offset):
    count = lax.axis_size(axis)
    pairs = [(i + offset, i) for i in range(count) if 0 <= i + offset < count]
    return lax.ppermute(block, axis, pairs)


def shift_from_2d(block, offset_x, offset_y):
    count_x = lax.axis_size("tx")
    count_y = lax.axis_size("ty")
    pairs = []
    for i in range(count_x):
        for j in range(count_y):
            si, sj = i + offset_x, j + offset_y
            if 0 <= si < count_x and 0 <= sj < count_y:
                pairs.append((si * count_y + sj, i * count_y + j))
    return lax.ppermute(block, ("tx", "ty"), pairs)


def coarse_ext(field):
    north = shift_from(field[-2:, :], "tx", -1)
    south = shift_from(field[:2, :], "tx", 1)
    west = shift_from(field[:, -2:], "ty", -1)
    east = shift_from(field[:, :2], "ty", 1)
    north_west = shift_from_2d(field[-2:, -2:], -1, -1)
    north_east = shift_from_2d(field[-2:, :2], -1, 1)
    south_west = shift_from_2d(field[:2, -2:], 1, -1)
    south_east = shift_from_2d(field[:2, :2], 1, 1)
    top = jnp.concatenate([north_west, north, north_east], axis=1)
    middle = jnp.concatenate([west, field, east], axis=1)
    bottom = jnp.concatenate([south_west, south, south_east], axis=1)
    return jnp.concatenate([top, middle, bottom], axis=0)


def operate(source_field, diagonal):
    above = shift_from(source_field, "layer", 1)
    below = shift_from(source_field, "layer", -1)
    north = shift_from(source_field[:, -1:, :], "tx", -1)
    south = shift_from(source_field[:, :1, :], "tx", 1)
    west = shift_from(source_field[:, :, -1:], "ty", -1)
    east = shift_from(source_field[:, :, :1], "ty", 1)
    lateral = (
        jnp.concatenate([source_field[:, 1:, :], south], axis=1)
        + jnp.concatenate([north, source_field[:, :-1, :]], axis=1)
        + jnp.concatenate([source_field[:, :, 1:], east], axis=2)
        + jnp.concatenate([west, source_field[:, :, :-1]], axis=2)
    )
    vertical = above + below
    return diagonal * source_field - lateral - VIA_CONDUCTANCE * vertical


def coarse_sweep(potential, coarse_rhs, coarse_diag, padded):
    beside = (
        padded[..., 2:, 1:-1]
        + padded[..., :-2, 1:-1]
        + padded[..., 1:-1, 2:]
        + padded[..., 1:-1, :-2]
    )
    return (
        potential
        + RELAXATION * (coarse_rhs - (coarse_diag * potential - COARSE_EDGE * beside)) / coarse_diag
    )


def restrict(source_field, gather):
    flat = source_field.reshape(1, -1)
    summed = jnp.dot(
        flat, gather, precision=lax.Precision.HIGHEST, preferred_element_type=jnp.float32
    )
    return summed.reshape(CGX, CGY)


def prolong(potential, gather, shape):
    spread = jnp.dot(
        gather,
        potential.reshape(-1),
        precision=lax.Precision.HIGHEST,
        preferred_element_type=jnp.float32,
    )
    return spread.reshape(shape)


def precondition(residual, diagonal, gather, diag_ext, inside_ext):
    coarse_rhs = coarse_ext(restrict(residual, gather))
    potential = jnp.where(inside_ext, RELAXATION * coarse_rhs / diag_ext, 0.0)
    for sweep_turn in range(SWEEPS - 1):
        potential = coarse_sweep(
            potential[1:-1, 1:-1], coarse_rhs[1:-1, 1:-1], diag_ext[1:-1, 1:-1], potential
        )
        coarse_rhs = coarse_rhs[1:-1, 1:-1]
        diag_ext = diag_ext[1:-1, 1:-1]
        inside_ext = inside_ext[1:-1, 1:-1]
        potential = jnp.where(inside_ext, potential, 0.0)
    return residual / diagonal + prolong(potential, gather, residual.shape)


def body(shunt_conductance, agg_map, slot_current, slot_node, slot_count):
    height = shunt_conductance.shape[1]
    breadth = shunt_conductance.shape[2]
    tile_count = slot_count.shape[3]
    capacity = slot_current.shape[4]
    live_mask = lax.broadcasted_iota(jnp.int32, slot_current.shape, 4) < slot_count[..., None]
    currents = jnp.where(live_mask, slot_current, jnp.zeros_like(slot_current))
    targets = slot_node.astype(jnp.float32)
    packed = jnp.stack(
        [currents.reshape(tile_count, capacity), targets.reshape(tile_count, capacity)], axis=1
    )
    arrived = lax.all_to_all(packed, ("tx", "ty"), split_axis=0, concat_axis=0, tiled=True)
    arrived_current = arrived[:, 0, :].reshape(-1)
    node_ids = arrived[:, 1, :].reshape(-1).astype(jnp.int32)
    row_hit = (
        (node_ids // breadth)[:, None] == lax.broadcasted_iota(jnp.int32, (1, height), 1)
    )
    col_hit = (
        (node_ids % breadth)[:, None] == lax.broadcasted_iota(jnp.int32, (1, breadth), 1)
    ).astype(jnp.float32)
    weighted_rows = jnp.where(row_hit, arrived_current[:, None], 0.0)
    sources = lax.dot_general(
        weighted_rows,
        col_hit,
        (((0,), (0,)), ((), ())),
        precision=lax.Precision.HIGHEST,
        preferred_element_type=jnp.float32,
    ).reshape(1, height, breadth)

    gather = (
        agg_map.reshape(-1)[:, None] == lax.broadcasted_iota(jnp.int32, (1, CGX * CGY), 1)
    ).astype(jnp.float32)
    diagonal = shunt_conductance + (4.0 + 2.0 * VIA_CONDUCTANCE)
    coarse_diag = 4.0 * COARSE_EDGE + restrict(shunt_conductance + 2.0 * VIA_CONDUCTANCE, gather)
    row_of = lax.axis_index("tx") * CGX - 2 + lax.broadcasted_iota(jnp.int32, (CGX + 4, CGY + 4), 0)
    col_of = lax.axis_index("ty") * CGY - 2 + lax.broadcasted_iota(jnp.int32, (CGX + 4, CGY + 4), 1)
    inside_ext = (
        (row_of >= 0)
        & (row_of < lax.axis_size("tx") * CGX)
        & (col_of >= 0)
        & (col_of < lax.axis_size("ty") * CGY)
    )
    diag_ext = jnp.where(inside_ext, coarse_ext(coarse_diag), 1.0)

    basis = [precondition(sources, diagonal, gather, diag_ext, inside_ext)]
    images = []
    for iteration in range(ITERS):
        images.append(operate(basis[-1], diagonal))
        if iteration + 1 < ITERS:
            basis.append(precondition(images[-1], diagonal, gather, diag_ext, inside_ext))
    residual_side = [sources] + images[: ITERS - 1]
    local = [jnp.sum(left * right) for left in residual_side for right in basis]
    local += [jnp.sum(left * right) for left in basis for right in images]
    sums = total(jnp.stack(local))
    gram_rz = sums[: ITERS * ITERS].reshape(ITERS, ITERS)
    gram_za = sums[ITERS * ITERS :].reshape(ITERS, ITERS)

    def form(coords_left, gram, coords_right):
        return jnp.dot(coords_left, jnp.dot(gram, coords_right, precision=lax.Precision.HIGHEST),
                       precision=lax.Precision.HIGHEST)

    unit = jnp.zeros((ITERS,), jnp.float32).at[0].set(1.0)
    residual_coords = jnp.zeros((ITERS + 1,), jnp.float32).at[0].set(1.0)
    voltage_coords = jnp.zeros((ITERS,), jnp.float32)
    direction = unit
    curv_now = form(residual_coords[:ITERS], gram_rz, residual_coords[:ITERS])
    for iteration in range(ITERS):
        energy = form(direction, gram_za, direction)
        step_size = curv_now / energy
        voltage_coords = voltage_coords + step_size * direction
        residual_coords = residual_coords.at[1:].add(-step_size * direction)
        if iteration + 1 < ITERS:
            curv_next = form(residual_coords[:ITERS], gram_rz, residual_coords[:ITERS])
            direction = residual_coords[:ITERS] + curv_next / curv_now * direction
            curv_now = curv_next
    voltage = voltage_coords[0] * basis[0]
    for index in range(1, ITERS):
        voltage = voltage + voltage_coords[index] * basis[index]
    residual = residual_coords[0] * sources
    for index in range(ITERS):
        residual = residual + residual_coords[index + 1] * images[index]
    return (voltage, residual)


def solution(mesh):
    in_specs = (
        P("layer", "tx", "ty"),
        P("layer", "tx", "ty"),
        P("layer", "tx", "ty", None, None),
        P("layer", "tx", "ty", None, None),
        P("layer", "tx", "ty", None),
    )
    out_specs = (P("layer", "tx", "ty"), P("layer", "tx", "ty"))
    return jax.shard_map(body, mesh=mesh, in_specs=in_specs, out_specs=out_specs, check_vma=False)
```

```python
import jax
import jax.numpy as jnp
from jax import lax
from jax.sharding import PartitionSpec as P

CGX = 8
CGY = 16
ITERS = 3
SWEEPS = 3


VIA_CONDUCTANCE = 0.5
COARSE_EDGE = 8.0
RELAXATION = 0.6
KRYLOV_SHIFT = 1.0


def total(vector):
    for axis in ("ty", "tx", "layer"):
        vector = lax.psum(vector, axis)
    return vector


def shift_from(block, axis, offset):
    count = lax.axis_size(axis)
    pairs = [(i + offset, i) for i in range(count) if 0 <= i + offset < count]
    return lax.ppermute(block, axis, pairs)


def shift_from_2d(block, offset_x, offset_y):
    count_x = lax.axis_size("tx")
    count_y = lax.axis_size("ty")
    pairs = []
    for i in range(count_x):
        for j in range(count_y):
            si, sj = i + offset_x, j + offset_y
            if 0 <= si < count_x and 0 <= sj < count_y:
                pairs.append((si * count_y + sj, i * count_y + j))
    return lax.ppermute(block, ("tx", "ty"), pairs)


def coarse_ext(field):
    north = shift_from(field[-2:, :], "tx", -1)
    south = shift_from(field[:2, :], "tx", 1)
    west = shift_from(field[:, -2:], "ty", -1)
    east = shift_from(field[:, :2], "ty", 1)
    north_west = shift_from_2d(field[-2:, -2:], -1, -1)
    north_east = shift_from_2d(field[-2:, :2], -1, 1)
    south_west = shift_from_2d(field[:2, -2:], 1, -1)
    south_east = shift_from_2d(field[:2, :2], 1, 1)
    top = jnp.concatenate([north_west, north, north_east], axis=1)
    middle = jnp.concatenate([west, field, east], axis=1)
    bottom = jnp.concatenate([south_west, south, south_east], axis=1)
    return jnp.concatenate([top, middle, bottom], axis=0)


def operate(source_field, diagonal):
    above = shift_from(source_field, "layer", 1)
    below = shift_from(source_field, "layer", -1)
    north = shift_from(source_field[:, -1:, :], "tx", -1)
    south = shift_from(source_field[:, :1, :], "tx", 1)
    west = shift_from(source_field[:, :, -1:], "ty", -1)
    east = shift_from(source_field[:, :, :1], "ty", 1)
    lateral = (
        jnp.concatenate([source_field[:, 1:, :], south], axis=1)
        + jnp.concatenate([north, source_field[:, :-1, :]], axis=1)
        + jnp.concatenate([source_field[:, :, 1:], east], axis=2)
        + jnp.concatenate([west, source_field[:, :, :-1]], axis=2)
    )
    vertical = above + below
    return diagonal * source_field - lateral - VIA_CONDUCTANCE * vertical


def coarse_sweep(potential, coarse_rhs, coarse_diag, padded):
    beside = (
        padded[..., 2:, 1:-1]
        + padded[..., :-2, 1:-1]
        + padded[..., 1:-1, 2:]
        + padded[..., 1:-1, :-2]
    )
    return (
        potential
        + RELAXATION * (coarse_rhs - (coarse_diag * potential - COARSE_EDGE * beside)) / coarse_diag
    )


def restrict(source_field, gather):
    flat = source_field.reshape(1, -1)
    summed = jnp.dot(
        flat, gather, precision=lax.Precision.HIGHEST, preferred_element_type=jnp.float32
    )
    return summed.reshape(CGX, CGY)


def prolong(potential, gather, shape):
    spread = jnp.dot(
        gather,
        potential.reshape(-1),
        precision=lax.Precision.HIGHEST,
        preferred_element_type=jnp.float32,
    )
    return spread.reshape(shape)


def precondition(residual, diagonal, gather, diag_ext, inside_ext):
    coarse_rhs = coarse_ext(restrict(residual, gather))
    potential = jnp.where(inside_ext, RELAXATION * coarse_rhs / diag_ext, 0.0)
    for sweep_turn in range(SWEEPS - 1):
        potential = coarse_sweep(
            potential[1:-1, 1:-1], coarse_rhs[1:-1, 1:-1], diag_ext[1:-1, 1:-1], potential
        )
        coarse_rhs = coarse_rhs[1:-1, 1:-1]
        diag_ext = diag_ext[1:-1, 1:-1]
        inside_ext = inside_ext[1:-1, 1:-1]
        potential = jnp.where(inside_ext, potential, 0.0)
    return residual / diagonal + prolong(potential, gather, residual.shape)


def body(shunt_conductance, agg_map, slot_current, slot_node, slot_count):
    height = shunt_conductance.shape[1]
    breadth = shunt_conductance.shape[2]
    tile_count = slot_count.shape[3]
    capacity = slot_current.shape[4]
    live_mask = lax.broadcasted_iota(jnp.int32, slot_current.shape, 4) < slot_count[..., None]
    currents = jnp.where(live_mask, slot_current, jnp.zeros_like(slot_current))
    targets = slot_node.astype(jnp.float32)
    packed = jnp.stack(
        [currents.reshape(tile_count, capacity), targets.reshape(tile_count, capacity)], axis=1
    )
    arrived = lax.all_to_all(packed, ("tx", "ty"), split_axis=0, concat_axis=0, tiled=True)
    arrived_current = arrived[:, 0, :].reshape(-1)
    node_ids = arrived[:, 1, :].reshape(-1).astype(jnp.int32)
    row_hit = (
        (node_ids // breadth)[:, None] == lax.broadcasted_iota(jnp.int32, (1, height), 1)
    )
    col_hit = (
        (node_ids % breadth)[:, None] == lax.broadcasted_iota(jnp.int32, (1, breadth), 1)
    ).astype(jnp.float32)
    weighted_rows = jnp.where(row_hit, arrived_current[:, None], 0.0)
    sources = lax.dot_general(
        weighted_rows,
        col_hit,
        (((0,), (0,)), ((), ())),
        precision=lax.Precision.HIGHEST,
        preferred_element_type=jnp.float32,
    ).reshape(1, height, breadth)

    gather = (
        agg_map.reshape(-1)[:, None] == lax.broadcasted_iota(jnp.int32, (1, CGX * CGY), 1)
    ).astype(jnp.float32)
    diagonal = shunt_conductance + (4.0 + 2.0 * VIA_CONDUCTANCE)
    coarse_diag = 4.0 * COARSE_EDGE + restrict(shunt_conductance + 2.0 * VIA_CONDUCTANCE, gather)
    row_of = lax.axis_index("tx") * CGX - 2 + lax.broadcasted_iota(jnp.int32, (CGX + 4, CGY + 4), 0)
    col_of = lax.axis_index("ty") * CGY - 2 + lax.broadcasted_iota(jnp.int32, (CGX + 4, CGY + 4), 1)
    inside_ext = (
        (row_of >= 0)
        & (row_of < lax.axis_size("tx") * CGX)
        & (col_of >= 0)
        & (col_of < lax.axis_size("ty") * CGY)
    )
    diag_ext = jnp.where(inside_ext, coarse_ext(coarse_diag), 1.0)

    basis = [precondition(sources, diagonal, gather, diag_ext, inside_ext)]
    images = []
    for iteration in range(ITERS):
        images.append(operate(basis[-1], diagonal))
        if iteration + 1 < ITERS:
            basis.append(
                precondition(images[-1], diagonal, gather, diag_ext, inside_ext)
                - KRYLOV_SHIFT * basis[-1]
            )
    residual_side = [sources] + images[: ITERS - 1]
    local = [jnp.sum(left * right) for left in residual_side for right in basis]
    local += [jnp.sum(left * right) for left in basis for right in images]
    sums = total(jnp.stack(local))
    gram_rz = sums[: ITERS * ITERS].reshape(ITERS, ITERS)
    gram_za = sums[ITERS * ITERS :].reshape(ITERS, ITERS)

    def form(coords_left, gram, coords_right):
        return jnp.dot(coords_left, jnp.dot(gram, coords_right, precision=lax.Precision.HIGHEST),
                       precision=lax.Precision.HIGHEST)

    unit = jnp.zeros((ITERS,), jnp.float32).at[0].set(1.0)
    residual_coords = jnp.zeros((ITERS + 1,), jnp.float32).at[0].set(1.0)
    voltage_coords = jnp.zeros((ITERS,), jnp.float32)
    direction = unit
    def smoothed_coords(coords):
        return coords[:ITERS] + KRYLOV_SHIFT * coords[1:]

    curv_now = form(residual_coords[:ITERS], gram_rz, smoothed_coords(residual_coords))
    for iteration in range(ITERS):
        energy = form(direction, gram_za, direction)
        step_size = curv_now / energy
        voltage_coords = voltage_coords + step_size * direction
        residual_coords = residual_coords.at[1:].add(-step_size * direction)
        if iteration + 1 < ITERS:
            curv_next = form(residual_coords[:ITERS], gram_rz, smoothed_coords(residual_coords))
            direction = smoothed_coords(residual_coords) + curv_next / curv_now * direction
            curv_now = curv_next
    voltage = voltage_coords[0] * basis[0]
    for index in range(1, ITERS):
        voltage = voltage + voltage_coords[index] * basis[index]
    residual = residual_coords[0] * sources
    for index in range(ITERS):
        residual = residual + residual_coords[index + 1] * images[index]
    return (voltage, residual)


def solution(mesh):
    in_specs = (
        P("layer", "tx", "ty"),
        P("layer", "tx", "ty"),
        P("layer", "tx", "ty", None, None),
        P("layer", "tx", "ty", None, None),
        P("layer", "tx", "ty", None),
    )
    out_specs = (P("layer", "tx", "ty"), P("layer", "tx", "ty"))
    return jax.shard_map(body, mesh=mesh, in_specs=in_specs, out_specs=out_specs, check_vma=False)
```

```python
import jax
import jax.numpy as jnp
from jax import lax
from jax.sharding import PartitionSpec as P

CGX = 8
CGY = 16
ITERS = 3
SWEEPS = 3


VIA_CONDUCTANCE = 0.5
COARSE_EDGE = 8.0
RELAXATION = 0.6
KRYLOV_SHIFT = 1.0


def total(vector):
    for axis in ("ty", "tx", "layer"):
        vector = lax.psum(vector, axis)
    return vector


def shift_from(block, axis, offset):
    count = lax.axis_size(axis)
    pairs = [(i + offset, i) for i in range(count) if 0 <= i + offset < count]
    return lax.ppermute(block, axis, pairs)


def shift_from_2d(block, offset_x, offset_y):
    count_x = lax.axis_size("tx")
    count_y = lax.axis_size("ty")
    pairs = []
    for i in range(count_x):
        for j in range(count_y):
            si, sj = i + offset_x, j + offset_y
            if 0 <= si < count_x and 0 <= sj < count_y:
                pairs.append((si * count_y + sj, i * count_y + j))
    return lax.ppermute(block, ("tx", "ty"), pairs)


def coarse_ext(field):
    north = shift_from(field[..., -2:, :], "tx", -1)
    south = shift_from(field[..., :2, :], "tx", 1)
    west = shift_from(field[..., :, -2:], "ty", -1)
    east = shift_from(field[..., :, :2], "ty", 1)
    north_west = shift_from_2d(field[..., -2:, -2:], -1, -1)
    north_east = shift_from_2d(field[..., -2:, :2], -1, 1)
    south_west = shift_from_2d(field[..., :2, -2:], 1, -1)
    south_east = shift_from_2d(field[..., :2, :2], 1, 1)
    top = jnp.concatenate([north_west, north, north_east], axis=-1)
    middle = jnp.concatenate([west, field, east], axis=-1)
    bottom = jnp.concatenate([south_west, south, south_east], axis=-1)
    return jnp.concatenate([top, middle, bottom], axis=-2)


def operate(source_field, diagonal):
    above = shift_from(source_field, "layer", 1)
    below = shift_from(source_field, "layer", -1)
    north = shift_from(source_field[:, -1:, :], "tx", -1)
    south = shift_from(source_field[:, :1, :], "tx", 1)
    west = shift_from(source_field[:, :, -1:], "ty", -1)
    east = shift_from(source_field[:, :, :1], "ty", 1)
    lateral = (
        jnp.concatenate([source_field[:, 1:, :], south], axis=1)
        + jnp.concatenate([north, source_field[:, :-1, :]], axis=1)
        + jnp.concatenate([source_field[:, :, 1:], east], axis=2)
        + jnp.concatenate([west, source_field[:, :, :-1]], axis=2)
    )
    vertical = above + below
    return diagonal * source_field - lateral - VIA_CONDUCTANCE * vertical


def coarse_sweep(potential, coarse_rhs, coarse_diag, padded):
    beside = (
        padded[..., 2:, 1:-1]
        + padded[..., :-2, 1:-1]
        + padded[..., 1:-1, 2:]
        + padded[..., 1:-1, :-2]
    )
    return (
        potential
        + RELAXATION * (coarse_rhs - (coarse_diag * potential - COARSE_EDGE * beside)) / coarse_diag
    )


def restrict(source_field, gather):
    flat = source_field.reshape(1, -1)
    summed = jnp.dot(
        flat, gather, precision=lax.Precision.HIGHEST, preferred_element_type=jnp.float32
    )
    return summed.reshape(CGX, CGY)


def prolong(potential, gather, shape):
    spread = jnp.dot(
        gather,
        potential.reshape(-1),
        precision=lax.Precision.HIGHEST,
        preferred_element_type=jnp.float32,
    )
    return spread.reshape(shape)


def precondition(residual, diagonal, gather, diag_ext, inside_ext, coarse_diag=None):
    coarse_rhs = restrict(residual, gather)
    if diag_ext is None:
        both = coarse_ext(jnp.stack([coarse_rhs, coarse_diag]))
        coarse_rhs = both[0]
        diag_ext = jnp.where(inside_ext, both[1], 1.0)
    else:
        coarse_rhs = coarse_ext(coarse_rhs)
    whole_diag = diag_ext
    potential = jnp.where(inside_ext, RELAXATION * coarse_rhs / diag_ext, 0.0)
    for sweep_turn in range(SWEEPS - 1):
        potential = coarse_sweep(
            potential[1:-1, 1:-1], coarse_rhs[1:-1, 1:-1], diag_ext[1:-1, 1:-1], potential
        )
        coarse_rhs = coarse_rhs[1:-1, 1:-1]
        diag_ext = diag_ext[1:-1, 1:-1]
        inside_ext = inside_ext[1:-1, 1:-1]
        potential = jnp.where(inside_ext, potential, 0.0)
    return residual / diagonal + prolong(potential, gather, residual.shape), whole_diag


def body(shunt_conductance, agg_map, slot_current, slot_node, slot_count):
    height = shunt_conductance.shape[1]
    breadth = shunt_conductance.shape[2]
    tile_count = slot_count.shape[3]
    capacity = slot_current.shape[4]
    live_mask = lax.broadcasted_iota(jnp.int32, slot_current.shape, 4) < slot_count[..., None]
    currents = jnp.where(live_mask, slot_current, jnp.zeros_like(slot_current))
    targets = slot_node.astype(jnp.float32)
    packed = jnp.stack(
        [currents.reshape(tile_count, capacity), targets.reshape(tile_count, capacity)], axis=1
    )
    arrived = lax.all_to_all(packed, ("tx", "ty"), split_axis=0, concat_axis=0, tiled=True)
    arrived_current = arrived[:, 0, :].reshape(-1)
    node_ids = arrived[:, 1, :].reshape(-1).astype(jnp.int32)
    row_hit = (
        (node_ids // breadth)[:, None] == lax.broadcasted_iota(jnp.int32, (1, height), 1)
    )
    col_hit = (
        (node_ids % breadth)[:, None] == lax.broadcasted_iota(jnp.int32, (1, breadth), 1)
    ).astype(jnp.float32)
    weighted_rows = jnp.where(row_hit, arrived_current[:, None], 0.0)
    sources = lax.dot_general(
        weighted_rows,
        col_hit,
        (((0,), (0,)), ((), ())),
        precision=lax.Precision.HIGHEST,
        preferred_element_type=jnp.float32,
    ).reshape(1, height, breadth)

    gather = (
        agg_map.reshape(-1)[:, None] == lax.broadcasted_iota(jnp.int32, (1, CGX * CGY), 1)
    ).astype(jnp.float32)
    diagonal = shunt_conductance + (4.0 + 2.0 * VIA_CONDUCTANCE)
    coarse_diag = 4.0 * COARSE_EDGE + restrict(shunt_conductance + 2.0 * VIA_CONDUCTANCE, gather)
    row_of = lax.axis_index("tx") * CGX - 2 + lax.broadcasted_iota(jnp.int32, (CGX + 4, CGY + 4), 0)
    col_of = lax.axis_index("ty") * CGY - 2 + lax.broadcasted_iota(jnp.int32, (CGX + 4, CGY + 4), 1)
    inside_ext = (
        (row_of >= 0)
        & (row_of < lax.axis_size("tx") * CGX)
        & (col_of >= 0)
        & (col_of < lax.axis_size("ty") * CGY)
    )

    first, diag_ext = precondition(sources, diagonal, gather, None, inside_ext, coarse_diag)
    basis = [first]
    images = []
    for iteration in range(ITERS):
        images.append(operate(basis[-1], diagonal))
        if iteration + 1 < ITERS:
            smoothed, diag_ext = precondition(images[-1], diagonal, gather, diag_ext, inside_ext)
            basis.append(smoothed - KRYLOV_SHIFT * basis[-1])
    residual_side = [sources] + images[: ITERS - 1]
    left = jnp.stack([field.reshape(-1) for field in residual_side + basis])
    right = jnp.stack([field.reshape(-1) for field in basis + images])
    local = lax.dot_general(
        left,
        right,
        (((1,), (1,)), ((), ())),
        precision=lax.Precision.HIGHEST,
        preferred_element_type=jnp.float32,
    )
    sums = total(
        jnp.concatenate([local[:ITERS, :ITERS].reshape(-1), local[ITERS:, ITERS:].reshape(-1)])
    ).reshape(2 * ITERS, ITERS)
    gram_rz = [[sums[i, j] for j in range(ITERS)] for i in range(ITERS)]
    gram_za = [[sums[ITERS + i, j] for j in range(ITERS)] for i in range(ITERS)]

    def form(coords_left, gram, coords_right):
        terms = [
            coords_left[i] * gram[i][j] * coords_right[j]
            for i in range(ITERS)
            for j in range(ITERS)
            if coords_left[i] is not None and coords_right[j] is not None
        ]
        result = terms[0]
        for term in terms[1:]:
            result = result + term
        return result

    def scaled_add(first_term, factor, second_term):
        if second_term is None:
            return first_term
        if first_term is None:
            return factor * second_term
        return first_term + factor * second_term

    def smoothed_coords(coords):
        return [
            scaled_add(coords[i], KRYLOV_SHIFT, coords[i + 1]) for i in range(ITERS)
        ]

    residual_coords = [1.0] + [None] * ITERS
    voltage_coords = [None] * ITERS
    direction = [1.0] + [None] * (ITERS - 1)
    curv_now = form(residual_coords, gram_rz, smoothed_coords(residual_coords))
    for iteration in range(ITERS):
        energy = form(direction, gram_za, direction)
        step_size = curv_now / energy
        voltage_coords = [
            scaled_add(voltage_coords[i], step_size, direction[i]) for i in range(ITERS)
        ]
        residual_coords = [residual_coords[0]] + [
            scaled_add(residual_coords[i + 1], -step_size, direction[i]) for i in range(ITERS)
        ]
        if iteration + 1 < ITERS:
            smoothed = smoothed_coords(residual_coords)
            curv_next = form(residual_coords, gram_rz, smoothed)
            ratio = curv_next / curv_now
            direction = [scaled_add(smoothed[i], ratio, direction[i]) for i in range(ITERS)]
            curv_now = curv_next
    voltage = voltage_coords[0] * basis[0]
    for index in range(1, ITERS):
        voltage = voltage + voltage_coords[index] * basis[index]
    residual = sources
    for index in range(ITERS):
        residual = residual + residual_coords[index + 1] * images[index]
    return (voltage, residual)


def solution(mesh):
    in_specs = (
        P("layer", "tx", "ty"),
        P("layer", "tx", "ty"),
        P("layer", "tx", "ty", None, None),
        P("layer", "tx", "ty", None, None),
        P("layer", "tx", "ty", None),
    )
    out_specs = (P("layer", "tx", "ty"), P("layer", "tx", "ty"))
    return jax.shard_map(body, mesh=mesh, in_specs=in_specs, out_specs=out_specs, check_vma=False)
```

```python
import jax
import jax.numpy as jnp
from jax import lax
from jax.sharding import PartitionSpec as P

CGX = 8
CGY = 16
ITERS = 3
SWEEPS = 3


VIA_CONDUCTANCE = 0.5
COARSE_EDGE = 8.0
RELAXATION = 0.6
KRYLOV_SHIFT = 1.0
LANES = 128


def total(vector):
    for axis in ("ty", "tx", "layer"):
        vector = lax.psum(vector, axis)
    return vector


def shift_from(block, axis, offset):
    count = lax.axis_size(axis)
    pairs = [(i + offset, i) for i in range(count) if 0 <= i + offset < count]
    return lax.ppermute(block, axis, pairs)


def shift_from_2d(block, offset_x, offset_y):
    count_x = lax.axis_size("tx")
    count_y = lax.axis_size("ty")
    pairs = []
    for i in range(count_x):
        for j in range(count_y):
            si, sj = i + offset_x, j + offset_y
            if 0 <= si < count_x and 0 <= sj < count_y:
                pairs.append((si * count_y + sj, i * count_y + j))
    return lax.ppermute(block, ("tx", "ty"), pairs)


def coarse_ext(field):
    north = shift_from(field[..., -2:, :], "tx", -1)
    south = shift_from(field[..., :2, :], "tx", 1)
    west = shift_from(field[..., :, -2:], "ty", -1)
    east = shift_from(field[..., :, :2], "ty", 1)
    north_west = shift_from_2d(field[..., -2:, -2:], -1, -1)
    north_east = shift_from_2d(field[..., -2:, :2], -1, 1)
    south_west = shift_from_2d(field[..., :2, -2:], 1, -1)
    south_east = shift_from_2d(field[..., :2, :2], 1, 1)
    top = jnp.concatenate([north_west, north, north_east], axis=-1)
    middle = jnp.concatenate([west, field, east], axis=-1)
    bottom = jnp.concatenate([south_west, south, south_east], axis=-1)
    return jnp.concatenate([top, middle, bottom], axis=-2)


def operate(source_field, diagonal):
    above = shift_from(source_field, "layer", 1)
    below = shift_from(source_field, "layer", -1)
    north = shift_from(source_field[:, -1:, :], "tx", -1)
    south = shift_from(source_field[:, :1, :], "tx", 1)
    west = shift_from(source_field[:, :, -1:], "ty", -1)
    east = shift_from(source_field[:, :, :1], "ty", 1)
    lateral = (
        jnp.concatenate([source_field[:, 1:, :], south], axis=1)
        + jnp.concatenate([north, source_field[:, :-1, :]], axis=1)
        + jnp.concatenate([source_field[:, :, 1:], east], axis=2)
        + jnp.concatenate([west, source_field[:, :, :-1]], axis=2)
    )
    vertical = above + below
    return diagonal * source_field - lateral - VIA_CONDUCTANCE * vertical


def coarse_sweep(potential, coarse_rhs, coarse_diag, padded):
    beside = (
        padded[..., 2:, 1:-1]
        + padded[..., :-2, 1:-1]
        + padded[..., 1:-1, 2:]
        + padded[..., 1:-1, :-2]
    )
    return (
        potential
        + RELAXATION * (coarse_rhs - (coarse_diag * potential - COARSE_EDGE * beside)) / coarse_diag
    )


def restrict(source_field, gather):
    flat = source_field.reshape(1, -1)
    summed = jnp.dot(
        flat, gather, precision=lax.Precision.HIGHEST, preferred_element_type=jnp.float32
    )
    return summed.reshape(CGX, CGY)


def prolong(potential, gather, shape):
    spread = jnp.dot(
        gather,
        potential.reshape(-1),
        precision=lax.Precision.HIGHEST,
        preferred_element_type=jnp.float32,
    )
    return spread.reshape(shape)


def precondition(residual, diagonal, gather, diag_ext, inside_ext, coarse_diag=None):
    coarse_rhs = restrict(residual, gather)
    if diag_ext is None:
        both = coarse_ext(jnp.stack([coarse_rhs, coarse_diag]))
        coarse_rhs = both[0]
        diag_ext = jnp.where(inside_ext, both[1], 1.0)
    else:
        coarse_rhs = coarse_ext(coarse_rhs)
    whole_diag = diag_ext
    potential = jnp.where(inside_ext, RELAXATION * coarse_rhs / diag_ext, 0.0)
    for sweep_turn in range(SWEEPS - 1):
        potential = coarse_sweep(
            potential[1:-1, 1:-1], coarse_rhs[1:-1, 1:-1], diag_ext[1:-1, 1:-1], potential
        )
        coarse_rhs = coarse_rhs[1:-1, 1:-1]
        diag_ext = diag_ext[1:-1, 1:-1]
        inside_ext = inside_ext[1:-1, 1:-1]
        potential = jnp.where(inside_ext, potential, 0.0)
    return residual / diagonal + prolong(potential, gather, residual.shape), whole_diag


def body(shunt_conductance, agg_map, slot_current, slot_node, slot_count):
    height = shunt_conductance.shape[1]
    breadth = shunt_conductance.shape[2]
    tile_count = slot_count.shape[3]
    capacity = slot_current.shape[4]
    live_mask = lax.broadcasted_iota(jnp.int32, slot_current.shape, 4) < slot_count[..., None]
    currents = jnp.where(live_mask, slot_current, jnp.zeros_like(slot_current))
    targets = slot_node.astype(jnp.float32)
    packed = jnp.stack(
        [currents.reshape(tile_count, capacity), targets.reshape(tile_count, capacity)], axis=1
    )
    arrived = lax.all_to_all(packed, ("tx", "ty"), split_axis=0, concat_axis=0, tiled=True)
    arrived_current = arrived[:, 0, :].reshape(-1)
    node_ids = arrived[:, 1, :].reshape(-1).astype(jnp.int32)
    row_hit = (
        (node_ids // breadth)[:, None] == lax.broadcasted_iota(jnp.int32, (1, height), 1)
    )
    col_hit = (
        (node_ids % breadth)[:, None] == lax.broadcasted_iota(jnp.int32, (1, breadth), 1)
    ).astype(jnp.float32)
    weighted_rows = jnp.where(row_hit, arrived_current[:, None], 0.0)
    sources = lax.dot_general(
        weighted_rows,
        col_hit,
        (((0,), (0,)), ((), ())),
        precision=lax.Precision.HIGHEST,
        preferred_element_type=jnp.float32,
    ).reshape(1, height, breadth)

    gather = (
        agg_map.reshape(-1)[:, None] == lax.broadcasted_iota(jnp.int32, (1, CGX * CGY), 1)
    ).astype(jnp.float32)
    diagonal = shunt_conductance + (4.0 + 2.0 * VIA_CONDUCTANCE)
    coarse_diag = 4.0 * COARSE_EDGE + restrict(shunt_conductance + 2.0 * VIA_CONDUCTANCE, gather)
    row_of = lax.axis_index("tx") * CGX - 2 + lax.broadcasted_iota(jnp.int32, (CGX + 4, CGY + 4), 0)
    col_of = lax.axis_index("ty") * CGY - 2 + lax.broadcasted_iota(jnp.int32, (CGX + 4, CGY + 4), 1)
    inside_ext = (
        (row_of >= 0)
        & (row_of < lax.axis_size("tx") * CGX)
        & (col_of >= 0)
        & (col_of < lax.axis_size("ty") * CGY)
    )

    first, diag_ext = precondition(sources, diagonal, gather, None, inside_ext, coarse_diag)
    basis = [first]
    images = []
    for iteration in range(ITERS):
        images.append(operate(basis[-1], diagonal))
        if iteration + 1 < ITERS:
            smoothed, diag_ext = precondition(images[-1], diagonal, gather, diag_ext, inside_ext)
            basis.append(smoothed - KRYLOV_SHIFT * basis[-1])
    residual_side = [sources] + images[: ITERS - 1]
    left = jnp.stack([field.reshape(-1) for field in residual_side + basis])
    right = jnp.stack([field.reshape(-1) for field in basis + images])
    local = lax.dot_general(
        left,
        right,
        (((1,), (1,)), ((), ())),
        precision=lax.Precision.HIGHEST,
        preferred_element_type=jnp.float32,
    )
    flat = jnp.concatenate([local[:ITERS, :ITERS].reshape(-1), local[ITERS:, ITERS:].reshape(-1)])
    lanes = total(jnp.broadcast_to(flat[:, None], (flat.shape[0], LANES)).reshape(-1))

    def entry(index):
        return lanes[index * LANES : (index + 1) * LANES]

    gram_rz = [[entry(i * ITERS + j) for j in range(ITERS)] for i in range(ITERS)]
    gram_za = [[entry((ITERS + i) * ITERS + j) for j in range(ITERS)] for i in range(ITERS)]

    def form(coords_left, gram, coords_right):
        terms = [
            coords_left[i] * gram[i][j] * coords_right[j]
            for i in range(ITERS)
            for j in range(ITERS)
            if coords_left[i] is not None and coords_right[j] is not None
        ]
        result = terms[0]
        for term in terms[1:]:
            result = result + term
        return result

    def scaled_add(first_term, factor, second_term):
        if second_term is None:
            return first_term
        if first_term is None:
            return factor * second_term
        return first_term + factor * second_term

    def smoothed_coords(coords):
        return [
            scaled_add(coords[i], KRYLOV_SHIFT, coords[i + 1]) for i in range(ITERS)
        ]

    residual_coords = [1.0] + [None] * ITERS
    voltage_coords = [None] * ITERS
    direction = [1.0] + [None] * (ITERS - 1)
    curv_now = form(residual_coords, gram_rz, smoothed_coords(residual_coords))
    for iteration in range(ITERS):
        energy = form(direction, gram_za, direction)
        step_size = curv_now / energy
        voltage_coords = [
            scaled_add(voltage_coords[i], step_size, direction[i]) for i in range(ITERS)
        ]
        residual_coords = [residual_coords[0]] + [
            scaled_add(residual_coords[i + 1], -step_size, direction[i]) for i in range(ITERS)
        ]
        if iteration + 1 < ITERS:
            smoothed = smoothed_coords(residual_coords)
            curv_next = form(residual_coords, gram_rz, smoothed)
            ratio = curv_next / curv_now
            direction = [scaled_add(smoothed[i], ratio, direction[i]) for i in range(ITERS)]
            curv_now = curv_next
    voltage = voltage_coords[0][0] * basis[0]
    for index in range(1, ITERS):
        voltage = voltage + voltage_coords[index][0] * basis[index]
    residual = sources
    for index in range(ITERS):
        residual = residual + residual_coords[index + 1][0] * images[index]
    return (voltage, residual)


def solution(mesh):
    in_specs = (
        P("layer", "tx", "ty"),
        P("layer", "tx", "ty"),
        P("layer", "tx", "ty", None, None),
        P("layer", "tx", "ty", None, None),
        P("layer", "tx", "ty", None),
    )
    out_specs = (P("layer", "tx", "ty"), P("layer", "tx", "ty"))
    return jax.shard_map(body, mesh=mesh, in_specs=in_specs, out_specs=out_specs, check_vma=False)
```

```python
import jax
import jax.numpy as jnp
from jax import lax
from jax.sharding import PartitionSpec as P

CGX = 8
CGY = 16
ITERS = 3
SWEEPS = 3


VIA_CONDUCTANCE = 0.5
COARSE_EDGE = 8.0
RELAXATION = 0.6
KRYLOV_SHIFT = 1.0
LANES = 128


def total(vector):
    for axis in ("ty", "tx", "layer"):
        vector = lax.psum(vector, axis)
    return vector


def shift_from(block, axis, offset):
    count = lax.axis_size(axis)
    pairs = [(i + offset, i) for i in range(count) if 0 <= i + offset < count]
    return lax.ppermute(block, axis, pairs)


def shift_from_2d(block, offset_x, offset_y):
    count_x = lax.axis_size("tx")
    count_y = lax.axis_size("ty")
    pairs = []
    for i in range(count_x):
        for j in range(count_y):
            si, sj = i + offset_x, j + offset_y
            if 0 <= si < count_x and 0 <= sj < count_y:
                pairs.append((si * count_y + sj, i * count_y + j))
    return lax.ppermute(block, ("tx", "ty"), pairs)


def coarse_ext(field):
    north = shift_from(field[..., -2:, :], "tx", -1)
    south = shift_from(field[..., :2, :], "tx", 1)
    west = shift_from(field[..., :, -2:], "ty", -1)
    east = shift_from(field[..., :, :2], "ty", 1)
    north_west = shift_from_2d(field[..., -2:, -2:], -1, -1)
    north_east = shift_from_2d(field[..., -2:, :2], -1, 1)
    south_west = shift_from_2d(field[..., :2, -2:], 1, -1)
    south_east = shift_from_2d(field[..., :2, :2], 1, 1)
    top = jnp.concatenate([north_west, north, north_east], axis=-1)
    middle = jnp.concatenate([west, field, east], axis=-1)
    bottom = jnp.concatenate([south_west, south, south_east], axis=-1)
    return jnp.concatenate([top, middle, bottom], axis=-2)


def operate(source_field, diagonal):
    above = shift_from(source_field, "layer", 1)
    below = shift_from(source_field, "layer", -1)
    north = shift_from(source_field[:, -1:, :], "tx", -1)
    south = shift_from(source_field[:, :1, :], "tx", 1)
    west = shift_from(source_field[:, :, -1:], "ty", -1)
    east = shift_from(source_field[:, :, :1], "ty", 1)
    lateral = (
        jnp.concatenate([source_field[:, 1:, :], south], axis=1)
        + jnp.concatenate([north, source_field[:, :-1, :]], axis=1)
        + jnp.concatenate([source_field[:, :, 1:], east], axis=2)
        + jnp.concatenate([west, source_field[:, :, :-1]], axis=2)
    )
    vertical = above + below
    return diagonal * source_field - lateral - VIA_CONDUCTANCE * vertical


def coarse_sweep(potential, coarse_rhs, coarse_diag, padded):
    beside = (
        padded[..., 2:, 1:-1]
        + padded[..., :-2, 1:-1]
        + padded[..., 1:-1, 2:]
        + padded[..., 1:-1, :-2]
    )
    return (
        potential
        + RELAXATION * (coarse_rhs - (coarse_diag * potential - COARSE_EDGE * beside)) / coarse_diag
    )


def restrict(source_field, gather):
    flat = source_field.reshape(1, -1)
    summed = jnp.dot(
        flat, gather, precision=lax.Precision.HIGHEST, preferred_element_type=jnp.float32
    )
    return summed.reshape(CGX, CGY)


def prolong(potential, gather, shape):
    spread = jnp.dot(
        gather,
        potential.reshape(-1),
        precision=lax.Precision.HIGHEST,
        preferred_element_type=jnp.float32,
    )
    return spread.reshape(shape)


def precondition(residual, diagonal, gather, diag_ext, inside_ext, coarse_diag=None):
    coarse_rhs = restrict(residual, gather)
    if diag_ext is None:
        both = coarse_ext(jnp.stack([coarse_rhs, coarse_diag]))
        coarse_rhs = both[0]
        diag_ext = jnp.where(inside_ext, both[1], 1.0)
    else:
        coarse_rhs = coarse_ext(coarse_rhs)
    whole_diag = diag_ext
    potential = jnp.where(inside_ext, RELAXATION * coarse_rhs / diag_ext, 0.0)
    for sweep_turn in range(SWEEPS - 1):
        potential = coarse_sweep(
            potential[1:-1, 1:-1], coarse_rhs[1:-1, 1:-1], diag_ext[1:-1, 1:-1], potential
        )
        coarse_rhs = coarse_rhs[1:-1, 1:-1]
        diag_ext = diag_ext[1:-1, 1:-1]
        inside_ext = inside_ext[1:-1, 1:-1]
        potential = jnp.where(inside_ext, potential, 0.0)
    return residual / diagonal + prolong(potential, gather, residual.shape), whole_diag


def body(shunt_conductance, agg_map, slot_current, slot_node, slot_count):
    height = shunt_conductance.shape[1]
    breadth = shunt_conductance.shape[2]
    tile_count = slot_count.shape[3]
    capacity = slot_current.shape[4]
    live_mask = lax.broadcasted_iota(jnp.int32, slot_current.shape, 4) < slot_count[..., None]
    currents = jnp.where(live_mask, slot_current, jnp.zeros_like(slot_current))
    targets = slot_node.astype(jnp.float32)
    packed = jnp.stack(
        [currents.reshape(tile_count, capacity), targets.reshape(tile_count, capacity)], axis=1
    )
    arrived = lax.all_to_all(packed, ("tx", "ty"), split_axis=0, concat_axis=0, tiled=True)
    arrived_current = arrived[:, 0, :].reshape(-1)
    node_ids = arrived[:, 1, :].reshape(-1).astype(jnp.int32)
    row_hit = (
        (node_ids // breadth)[:, None] == lax.broadcasted_iota(jnp.int32, (1, height), 1)
    )
    col_hit = (
        (node_ids % breadth)[:, None] == lax.broadcasted_iota(jnp.int32, (1, breadth), 1)
    ).astype(jnp.float32)
    weighted_rows = jnp.where(row_hit, arrived_current[:, None], 0.0)
    sources = lax.dot_general(
        weighted_rows,
        col_hit,
        (((0,), (0,)), ((), ())),
        precision=lax.Precision.HIGHEST,
        preferred_element_type=jnp.float32,
    ).reshape(1, height, breadth)

    gather = (
        agg_map.reshape(-1)[:, None] == lax.broadcasted_iota(jnp.int32, (1, CGX * CGY), 1)
    ).astype(jnp.float32)
    diagonal = shunt_conductance + (4.0 + 2.0 * VIA_CONDUCTANCE)
    coarse_diag = 4.0 * COARSE_EDGE + restrict(shunt_conductance + 2.0 * VIA_CONDUCTANCE, gather)
    row_of = lax.axis_index("tx") * CGX - 2 + lax.broadcasted_iota(jnp.int32, (CGX + 4, CGY + 4), 0)
    col_of = lax.axis_index("ty") * CGY - 2 + lax.broadcasted_iota(jnp.int32, (CGX + 4, CGY + 4), 1)
    inside_ext = (
        (row_of >= 0)
        & (row_of < lax.axis_size("tx") * CGX)
        & (col_of >= 0)
        & (col_of < lax.axis_size("ty") * CGY)
    )

    first, diag_ext = precondition(sources, diagonal, gather, None, inside_ext, coarse_diag)
    basis = [first]
    images = []
    for iteration in range(ITERS):
        images.append(operate(basis[-1], diagonal))
        if iteration + 1 < ITERS:
            smoothed, diag_ext = precondition(images[-1], diagonal, gather, diag_ext, inside_ext)
            basis.append(smoothed - KRYLOV_SHIFT * basis[-1])
    residual_side = [sources] + images[: ITERS - 1]
    left = jnp.stack([field.reshape(-1) for field in residual_side + basis])
    right = jnp.stack([field.reshape(-1) for field in basis + images])
    local = lax.dot_general(
        left,
        right,
        (((1,), (1,)), ((), ())),
        precision=lax.Precision.HIGHEST,
        preferred_element_type=jnp.float32,
    )
    flat = jnp.concatenate([local[:ITERS, :ITERS].reshape(-1), local[ITERS:, ITERS:].reshape(-1)])
    lanes = lax.optimization_barrier(
        jnp.broadcast_to(total(flat)[:, None], (flat.shape[0], LANES))
    ).reshape(-1)

    def entry(index):
        return lanes[index * LANES : (index + 1) * LANES]

    gram_rz = [[entry(i * ITERS + j) for j in range(ITERS)] for i in range(ITERS)]
    gram_za = [[entry((ITERS + i) * ITERS + j) for j in range(ITERS)] for i in range(ITERS)]

    def form(coords_left, gram, coords_right):
        terms = [
            coords_left[i] * gram[i][j] * coords_right[j]
            for i in range(ITERS)
            for j in range(ITERS)
            if coords_left[i] is not None and coords_right[j] is not None
        ]
        result = terms[0]
        for term in terms[1:]:
            result = result + term
        return result

    def scaled_add(first_term, factor, second_term):
        if second_term is None:
            return first_term
        if first_term is None:
            return factor * second_term
        return first_term + factor * second_term

    def smoothed_coords(coords):
        return [
            scaled_add(coords[i], KRYLOV_SHIFT, coords[i + 1]) for i in range(ITERS)
        ]

    residual_coords = [1.0] + [None] * ITERS
    voltage_coords = [None] * ITERS
    direction = [1.0] + [None] * (ITERS - 1)
    curv_now = form(residual_coords, gram_rz, smoothed_coords(residual_coords))
    for iteration in range(ITERS):
        energy = form(direction, gram_za, direction)
        step_size = curv_now / energy
        voltage_coords = [
            scaled_add(voltage_coords[i], step_size, direction[i]) for i in range(ITERS)
        ]
        residual_coords = [residual_coords[0]] + [
            scaled_add(residual_coords[i + 1], -step_size, direction[i]) for i in range(ITERS)
        ]
        if iteration + 1 < ITERS:
            smoothed = smoothed_coords(residual_coords)
            curv_next = form(residual_coords, gram_rz, smoothed)
            ratio = curv_next / curv_now
            direction = [scaled_add(smoothed[i], ratio, direction[i]) for i in range(ITERS)]
            curv_now = curv_next
    voltage = voltage_coords[0][0] * basis[0]
    for index in range(1, ITERS):
        voltage = voltage + voltage_coords[index][0] * basis[index]
    residual = sources
    for index in range(ITERS):
        residual = residual + residual_coords[index + 1][0] * images[index]
    return (voltage, residual)


def solution(mesh):
    in_specs = (
        P("layer", "tx", "ty"),
        P("layer", "tx", "ty"),
        P("layer", "tx", "ty", None, None),
        P("layer", "tx", "ty", None, None),
        P("layer", "tx", "ty", None),
    )
    out_specs = (P("layer", "tx", "ty"), P("layer", "tx", "ty"))
    return jax.shard_map(body, mesh=mesh, in_specs=in_specs, out_specs=out_specs, check_vma=False)
```

```python
import jax
import jax.numpy as jnp
from jax import lax
from jax.sharding import PartitionSpec as P

CGX = 8
CGY = 16
ITERS = 3
SWEEPS = 3


VIA_CONDUCTANCE = 0.5
COARSE_EDGE = 8.0
RELAXATION = 0.6
KRYLOV_SHIFT = 1.0
LANES = 128


def total(vector):
    for axis in ("ty", "tx", "layer"):
        vector = lax.psum(vector, axis)
    return vector


def shift_from(block, axis, offset):
    count = lax.axis_size(axis)
    pairs = [(i + offset, i) for i in range(count) if 0 <= i + offset < count]
    return lax.ppermute(block, axis, pairs)


def shift_from_2d(block, offset_x, offset_y):
    count_x = lax.axis_size("tx")
    count_y = lax.axis_size("ty")
    pairs = []
    for i in range(count_x):
        for j in range(count_y):
            si, sj = i + offset_x, j + offset_y
            if 0 <= si < count_x and 0 <= sj < count_y:
                pairs.append((si * count_y + sj, i * count_y + j))
    return lax.ppermute(block, ("tx", "ty"), pairs)


def coarse_ext(field):
    north = shift_from(field[..., -2:, :], "tx", -1)
    south = shift_from(field[..., :2, :], "tx", 1)
    rows = jnp.concatenate([north, field, south], axis=-2)
    west = shift_from(rows[..., :, -2:], "ty", -1)
    east = shift_from(rows[..., :, :2], "ty", 1)
    return jnp.concatenate([west, rows, east], axis=-1)


def operate(source_field, diagonal):
    above = shift_from(source_field, "layer", 1)
    below = shift_from(source_field, "layer", -1)
    north = shift_from(source_field[:, -1:, :], "tx", -1)
    south = shift_from(source_field[:, :1, :], "tx", 1)
    west = shift_from(source_field[:, :, -1:], "ty", -1)
    east = shift_from(source_field[:, :, :1], "ty", 1)
    lateral = (
        jnp.concatenate([source_field[:, 1:, :], south], axis=1)
        + jnp.concatenate([north, source_field[:, :-1, :]], axis=1)
        + jnp.concatenate([source_field[:, :, 1:], east], axis=2)
        + jnp.concatenate([west, source_field[:, :, :-1]], axis=2)
    )
    vertical = above + below
    return diagonal * source_field - lateral - VIA_CONDUCTANCE * vertical


def coarse_sweep(potential, coarse_rhs, coarse_diag, padded):
    beside = (
        padded[..., 2:, 1:-1]
        + padded[..., :-2, 1:-1]
        + padded[..., 1:-1, 2:]
        + padded[..., 1:-1, :-2]
    )
    return (
        potential
        + RELAXATION * (coarse_rhs - (coarse_diag * potential - COARSE_EDGE * beside)) / coarse_diag
    )


def restrict(source_field, gather):
    flat = source_field.reshape(1, -1)
    summed = jnp.dot(
        flat, gather, precision=lax.Precision.HIGHEST, preferred_element_type=jnp.float32
    )
    return summed.reshape(CGX, CGY)


def prolong(potential, gather, shape):
    spread = jnp.dot(
        gather,
        potential.reshape(-1),
        precision=lax.Precision.HIGHEST,
        preferred_element_type=jnp.float32,
    )
    return spread.reshape(shape)


def precondition(residual, diagonal, gather, diag_ext, inside_ext, coarse_diag=None):
    coarse_rhs = restrict(residual, gather)
    if diag_ext is None:
        both = coarse_ext(jnp.stack([coarse_rhs, coarse_diag]))
        coarse_rhs = both[0]
        diag_ext = jnp.where(inside_ext, both[1], 1.0)
    else:
        coarse_rhs = coarse_ext(coarse_rhs)
    whole_diag = diag_ext
    potential = jnp.where(inside_ext, RELAXATION * coarse_rhs / diag_ext, 0.0)
    for sweep_turn in range(SWEEPS - 1):
        potential = coarse_sweep(
            potential[1:-1, 1:-1], coarse_rhs[1:-1, 1:-1], diag_ext[1:-1, 1:-1], potential
        )
        coarse_rhs = coarse_rhs[1:-1, 1:-1]
        diag_ext = diag_ext[1:-1, 1:-1]
        inside_ext = inside_ext[1:-1, 1:-1]
        potential = jnp.where(inside_ext, potential, 0.0)
    return residual / diagonal + prolong(potential, gather, residual.shape), whole_diag


def body(shunt_conductance, agg_map, slot_current, slot_node, slot_count):
    height = shunt_conductance.shape[1]
    breadth = shunt_conductance.shape[2]
    tile_count = slot_count.shape[3]
    capacity = slot_current.shape[4]
    live_mask = lax.broadcasted_iota(jnp.int32, slot_current.shape, 4) < slot_count[..., None]
    currents = jnp.where(live_mask, slot_current, jnp.zeros_like(slot_current))
    targets = slot_node.astype(jnp.float32)
    packed = jnp.stack(
        [currents.reshape(tile_count, capacity), targets.reshape(tile_count, capacity)], axis=1
    )
    arrived = lax.all_to_all(packed, ("tx", "ty"), split_axis=0, concat_axis=0, tiled=True)
    arrived_current = arrived[:, 0, :].reshape(-1)
    node_ids = arrived[:, 1, :].reshape(-1).astype(jnp.int32)
    row_hit = (
        (node_ids // breadth)[:, None] == lax.broadcasted_iota(jnp.int32, (1, height), 1)
    )
    col_hit = (
        (node_ids % breadth)[:, None] == lax.broadcasted_iota(jnp.int32, (1, breadth), 1)
    ).astype(jnp.float32)
    weighted_rows = jnp.where(row_hit, arrived_current[:, None], 0.0)
    sources = lax.dot_general(
        weighted_rows,
        col_hit,
        (((0,), (0,)), ((), ())),
        precision=lax.Precision.HIGHEST,
        preferred_element_type=jnp.float32,
    ).reshape(1, height, breadth)

    gather = (
        agg_map.reshape(-1)[:, None] == lax.broadcasted_iota(jnp.int32, (1, CGX * CGY), 1)
    ).astype(jnp.float32)
    diagonal = shunt_conductance + (4.0 + 2.0 * VIA_CONDUCTANCE)
    coarse_diag = 4.0 * COARSE_EDGE + restrict(shunt_conductance + 2.0 * VIA_CONDUCTANCE, gather)
    row_of = lax.axis_index("tx") * CGX - 2 + lax.broadcasted_iota(jnp.int32, (CGX + 4, CGY + 4), 0)
    col_of = lax.axis_index("ty") * CGY - 2 + lax.broadcasted_iota(jnp.int32, (CGX + 4, CGY + 4), 1)
    inside_ext = (
        (row_of >= 0)
        & (row_of < lax.axis_size("tx") * CGX)
        & (col_of >= 0)
        & (col_of < lax.axis_size("ty") * CGY)
    )

    first, diag_ext = precondition(sources, diagonal, gather, None, inside_ext, coarse_diag)
    basis = [first]
    images = []
    for iteration in range(ITERS):
        images.append(operate(basis[-1], diagonal))
        if iteration + 1 < ITERS:
            smoothed, diag_ext = precondition(images[-1], diagonal, gather, diag_ext, inside_ext)
            basis.append(smoothed - KRYLOV_SHIFT * basis[-1])
    residual_side = [sources] + images[: ITERS - 1]
    left = jnp.stack([field.reshape(-1) for field in residual_side + basis])
    right = jnp.stack([field.reshape(-1) for field in basis + images])
    local = lax.dot_general(
        left,
        right,
        (((1,), (1,)), ((), ())),
        precision=lax.Precision.HIGHEST,
        preferred_element_type=jnp.float32,
    )
    flat = jnp.concatenate([local[:ITERS, :ITERS].reshape(-1), local[ITERS:, ITERS:].reshape(-1)])
    lanes = lax.optimization_barrier(
        jnp.broadcast_to(total(flat)[:, None], (flat.shape[0], LANES))
    ).reshape(-1)

    def entry(index):
        return lanes[index * LANES : (index + 1) * LANES]

    gram_rz = [[entry(i * ITERS + j) for j in range(ITERS)] for i in range(ITERS)]
    gram_za = [[entry((ITERS + i) * ITERS + j) for j in range(ITERS)] for i in range(ITERS)]

    def form(coords_left, gram, coords_right):
        terms = [
            coords_left[i] * gram[i][j] * coords_right[j]
            for i in range(ITERS)
            for j in range(ITERS)
            if coords_left[i] is not None and coords_right[j] is not None
        ]
        result = terms[0]
        for term in terms[1:]:
            result = result + term
        return result

    def scaled_add(first_term, factor, second_term):
        if second_term is None:
            return first_term
        if first_term is None:
            return factor * second_term
        return first_term + factor * second_term

    def smoothed_coords(coords):
        return [
            scaled_add(coords[i], KRYLOV_SHIFT, coords[i + 1]) for i in range(ITERS)
        ]

    residual_coords = [1.0] + [None] * ITERS
    voltage_coords = [None] * ITERS
    direction = [1.0] + [None] * (ITERS - 1)
    curv_now = form(residual_coords, gram_rz, smoothed_coords(residual_coords))
    for iteration in range(ITERS):
        energy = form(direction, gram_za, direction)
        step_size = curv_now / energy
        voltage_coords = [
            scaled_add(voltage_coords[i], step_size, direction[i]) for i in range(ITERS)
        ]
        residual_coords = [residual_coords[0]] + [
            scaled_add(residual_coords[i + 1], -step_size, direction[i]) for i in range(ITERS)
        ]
        if iteration + 1 < ITERS:
            smoothed = smoothed_coords(residual_coords)
            curv_next = form(residual_coords, gram_rz, smoothed)
            ratio = curv_next / curv_now
            direction = [scaled_add(smoothed[i], ratio, direction[i]) for i in range(ITERS)]
            curv_now = curv_next
    voltage = voltage_coords[0][0] * basis[0]
    for index in range(1, ITERS):
        voltage = voltage + voltage_coords[index][0] * basis[index]
    residual = sources
    for index in range(ITERS):
        residual = residual + residual_coords[index + 1][0] * images[index]
    return (voltage, residual)


def solution(mesh):
    in_specs = (
        P("layer", "tx", "ty"),
        P("layer", "tx", "ty"),
        P("layer", "tx", "ty", None, None),
        P("layer", "tx", "ty", None, None),
        P("layer", "tx", "ty", None),
    )
    out_specs = (P("layer", "tx", "ty"), P("layer", "tx", "ty"))
    return jax.shard_map(body, mesh=mesh, in_specs=in_specs, out_specs=out_specs, check_vma=False)
```

```python
import jax
import jax.numpy as jnp
from jax import lax
from jax.sharding import PartitionSpec as P

CGX = 8
CGY = 16
ITERS = 3
SWEEPS = 3


VIA_CONDUCTANCE = 0.5
COARSE_EDGE = 8.0
RELAXATION = 0.6
KRYLOV_SHIFT = 1.0
LANES = 128


def total(vector):
    for axis in ("ty", "tx", "layer"):
        vector = lax.psum(vector, axis)
    return vector


def shift_from(block, axis, offset):
    count = lax.axis_size(axis)
    pairs = [((i + offset) % count, i) for i in range(count)]
    moved = lax.ppermute(block, axis, pairs)
    source = lax.axis_index(axis) + offset
    return jnp.where((source >= 0) & (source < count), moved, jnp.zeros_like(moved))


def shift_from_2d(block, offset_x, offset_y):
    count_x = lax.axis_size("tx")
    count_y = lax.axis_size("ty")
    pairs = []
    for i in range(count_x):
        for j in range(count_y):
            si, sj = i + offset_x, j + offset_y
            if 0 <= si < count_x and 0 <= sj < count_y:
                pairs.append((si * count_y + sj, i * count_y + j))
    return lax.ppermute(block, ("tx", "ty"), pairs)


def coarse_ext(field):
    north = shift_from(field[..., -2:, :], "tx", -1)
    south = shift_from(field[..., :2, :], "tx", 1)
    rows = jnp.concatenate([north, field, south], axis=-2)
    west = shift_from(rows[..., :, -2:], "ty", -1)
    east = shift_from(rows[..., :, :2], "ty", 1)
    return jnp.concatenate([west, rows, east], axis=-1)


def operate(source_field, diagonal):
    above = shift_from(source_field, "layer", 1)
    below = shift_from(source_field, "layer", -1)
    north = shift_from(source_field[:, -1:, :], "tx", -1)
    south = shift_from(source_field[:, :1, :], "tx", 1)
    west = shift_from(source_field[:, :, -1:], "ty", -1)
    east = shift_from(source_field[:, :, :1], "ty", 1)
    lateral = (
        jnp.concatenate([source_field[:, 1:, :], south], axis=1)
        + jnp.concatenate([north, source_field[:, :-1, :]], axis=1)
        + jnp.concatenate([source_field[:, :, 1:], east], axis=2)
        + jnp.concatenate([west, source_field[:, :, :-1]], axis=2)
    )
    vertical = above + below
    return diagonal * source_field - lateral - VIA_CONDUCTANCE * vertical


def coarse_sweep(potential, coarse_rhs, coarse_diag, padded):
    beside = (
        padded[..., 2:, 1:-1]
        + padded[..., :-2, 1:-1]
        + padded[..., 1:-1, 2:]
        + padded[..., 1:-1, :-2]
    )
    return (
        potential
        + RELAXATION * (coarse_rhs - (coarse_diag * potential - COARSE_EDGE * beside)) / coarse_diag
    )


def restrict(source_field, gather):
    flat = source_field.reshape(1, -1)
    summed = jnp.dot(
        flat, gather, precision=lax.Precision.HIGHEST, preferred_element_type=jnp.float32
    )
    return summed.reshape(CGX, CGY)


def prolong(potential, gather, shape):
    spread = jnp.dot(
        gather,
        potential.reshape(-1),
        precision=lax.Precision.HIGHEST,
        preferred_element_type=jnp.float32,
    )
    return spread.reshape(shape)


def precondition(residual, diagonal, gather, diag_ext, inside_ext, coarse_diag=None):
    coarse_rhs = restrict(residual, gather)
    if diag_ext is None:
        both = coarse_ext(jnp.stack([coarse_rhs, coarse_diag]))
        coarse_rhs = both[0]
        diag_ext = jnp.where(inside_ext, both[1], 1.0)
    else:
        coarse_rhs = coarse_ext(coarse_rhs)
    whole_diag = diag_ext
    potential = jnp.where(inside_ext, RELAXATION * coarse_rhs / diag_ext, 0.0)
    for sweep_turn in range(SWEEPS - 1):
        potential = coarse_sweep(
            potential[1:-1, 1:-1], coarse_rhs[1:-1, 1:-1], diag_ext[1:-1, 1:-1], potential
        )
        coarse_rhs = coarse_rhs[1:-1, 1:-1]
        diag_ext = diag_ext[1:-1, 1:-1]
        inside_ext = inside_ext[1:-1, 1:-1]
        potential = jnp.where(inside_ext, potential, 0.0)
    return residual / diagonal + prolong(potential, gather, residual.shape), whole_diag


def body(shunt_conductance, agg_map, slot_current, slot_node, slot_count):
    height = shunt_conductance.shape[1]
    breadth = shunt_conductance.shape[2]
    tile_count = slot_count.shape[3]
    capacity = slot_current.shape[4]
    live_mask = lax.broadcasted_iota(jnp.int32, slot_current.shape, 4) < slot_count[..., None]
    currents = jnp.where(live_mask, slot_current, jnp.zeros_like(slot_current))
    targets = slot_node.astype(jnp.float32)
    packed = jnp.stack(
        [currents.reshape(tile_count, capacity), targets.reshape(tile_count, capacity)], axis=1
    )
    arrived = lax.all_to_all(packed, ("tx", "ty"), split_axis=0, concat_axis=0, tiled=True)
    arrived_current = arrived[:, 0, :].reshape(-1)
    node_ids = arrived[:, 1, :].reshape(-1).astype(jnp.int32)
    row_hit = (
        (node_ids // breadth)[:, None] == lax.broadcasted_iota(jnp.int32, (1, height), 1)
    )
    col_hit = (
        (node_ids % breadth)[:, None] == lax.broadcasted_iota(jnp.int32, (1, breadth), 1)
    ).astype(jnp.float32)
    weighted_rows = jnp.where(row_hit, arrived_current[:, None], 0.0)
    sources = lax.dot_general(
        weighted_rows,
        col_hit,
        (((0,), (0,)), ((), ())),
        precision=lax.Precision.HIGHEST,
        preferred_element_type=jnp.float32,
    ).reshape(1, height, breadth)

    gather = (
        agg_map.reshape(-1)[:, None] == lax.broadcasted_iota(jnp.int32, (1, CGX * CGY), 1)
    ).astype(jnp.float32)
    diagonal = shunt_conductance + (4.0 + 2.0 * VIA_CONDUCTANCE)
    coarse_diag = 4.0 * COARSE_EDGE + restrict(shunt_conductance + 2.0 * VIA_CONDUCTANCE, gather)
    row_of = lax.axis_index("tx") * CGX - 2 + lax.broadcasted_iota(jnp.int32, (CGX + 4, CGY + 4), 0)
    col_of = lax.axis_index("ty") * CGY - 2 + lax.broadcasted_iota(jnp.int32, (CGX + 4, CGY + 4), 1)
    inside_ext = (
        (row_of >= 0)
        & (row_of < lax.axis_size("tx") * CGX)
        & (col_of >= 0)
        & (col_of < lax.axis_size("ty") * CGY)
    )

    first, diag_ext = precondition(sources, diagonal, gather, None, inside_ext, coarse_diag)
    basis = [first]
    images = []
    for iteration in range(ITERS):
        images.append(operate(basis[-1], diagonal))
        if iteration + 1 < ITERS:
            smoothed, diag_ext = precondition(images[-1], diagonal, gather, diag_ext, inside_ext)
            basis.append(smoothed - KRYLOV_SHIFT * basis[-1])
    residual_side = [sources] + images[: ITERS - 1]
    left = jnp.stack([field.reshape(-1) for field in residual_side + basis])
    right = jnp.stack([field.reshape(-1) for field in basis + images])
    local = lax.dot_general(
        left,
        right,
        (((1,), (1,)), ((), ())),
        precision=lax.Precision.HIGHEST,
        preferred_element_type=jnp.float32,
    )
    flat = jnp.concatenate([local[:ITERS, :ITERS].reshape(-1), local[ITERS:, ITERS:].reshape(-1)])
    lanes = lax.optimization_barrier(
        jnp.broadcast_to(total(flat)[:, None], (flat.shape[0], LANES))
    ).reshape(-1)

    def entry(index):
        return lanes[index * LANES : (index + 1) * LANES]

    gram_rz = [[entry(i * ITERS + j) for j in range(ITERS)] for i in range(ITERS)]
    gram_za = [[entry((ITERS + i) * ITERS + j) for j in range(ITERS)] for i in range(ITERS)]

    def form(coords_left, gram, coords_right):
        terms = [
            coords_left[i] * gram[i][j] * coords_right[j]
            for i in range(ITERS)
            for j in range(ITERS)
            if coords_left[i] is not None and coords_right[j] is not None
        ]
        result = terms[0]
        for term in terms[1:]:
            result = result + term
        return result

    def scaled_add(first_term, factor, second_term):
        if second_term is None:
            return first_term
        if first_term is None:
            return factor * second_term
        return first_term + factor * second_term

    def smoothed_coords(coords):
        return [
            scaled_add(coords[i], KRYLOV_SHIFT, coords[i + 1]) for i in range(ITERS)
        ]

    residual_coords = [1.0] + [None] * ITERS
    voltage_coords = [None] * ITERS
    direction = [1.0] + [None] * (ITERS - 1)
    curv_now = form(residual_coords, gram_rz, smoothed_coords(residual_coords))
    for iteration in range(ITERS):
        energy = form(direction, gram_za, direction)
        step_size = curv_now / energy
        voltage_coords = [
            scaled_add(voltage_coords[i], step_size, direction[i]) for i in range(ITERS)
        ]
        residual_coords = [residual_coords[0]] + [
            scaled_add(residual_coords[i + 1], -step_size, direction[i]) for i in range(ITERS)
        ]
        if iteration + 1 < ITERS:
            smoothed = smoothed_coords(residual_coords)
            curv_next = form(residual_coords, gram_rz, smoothed)
            ratio = curv_next / curv_now
            direction = [scaled_add(smoothed[i], ratio, direction[i]) for i in range(ITERS)]
            curv_now = curv_next
    voltage = voltage_coords[0][0] * basis[0]
    for index in range(1, ITERS):
        voltage = voltage + voltage_coords[index][0] * basis[index]
    residual = sources
    for index in range(ITERS):
        residual = residual + residual_coords[index + 1][0] * images[index]
    return (voltage, residual)


def solution(mesh):
    in_specs = (
        P("layer", "tx", "ty"),
        P("layer", "tx", "ty"),
        P("layer", "tx", "ty", None, None),
        P("layer", "tx", "ty", None, None),
        P("layer", "tx", "ty", None),
    )
    out_specs = (P("layer", "tx", "ty"), P("layer", "tx", "ty"))
    return jax.shard_map(body, mesh=mesh, in_specs=in_specs, out_specs=out_specs, check_vma=False)
```

```python
import jax
import jax.numpy as jnp
from jax import lax
from jax.sharding import PartitionSpec as P

CGX = 8
CGY = 16
ITERS = 3
SWEEPS = 3


VIA_CONDUCTANCE = 0.5
COARSE_EDGE = 8.0
RELAXATION = 0.6
KRYLOV_SHIFT = 1.0
LANES = 128


def total(vector):
    for axis in ("layer", "tx", "ty"):
        vector = lax.psum(vector, axis)
    return vector


def shift_from(block, axis, offset):
    count = lax.axis_size(axis)
    pairs = [((i + offset) % count, i) for i in range(count)]
    moved = lax.ppermute(block, axis, pairs)
    source = lax.axis_index(axis) + offset
    return jnp.where((source >= 0) & (source < count), moved, jnp.zeros_like(moved))


def shift_from_2d(block, offset_x, offset_y):
    count_x = lax.axis_size("tx")
    count_y = lax.axis_size("ty")
    pairs = []
    for i in range(count_x):
        for j in range(count_y):
            si, sj = i + offset_x, j + offset_y
            if 0 <= si < count_x and 0 <= sj < count_y:
                pairs.append((si * count_y + sj, i * count_y + j))
    return lax.ppermute(block, ("tx", "ty"), pairs)


def coarse_ext(field):
    north = shift_from(field[..., -2:, :], "tx", -1)
    south = shift_from(field[..., :2, :], "tx", 1)
    rows = jnp.concatenate([north, field, south], axis=-2)
    west = shift_from(rows[..., :, -2:], "ty", -1)
    east = shift_from(rows[..., :, :2], "ty", 1)
    return jnp.concatenate([west, rows, east], axis=-1)


def operate(source_field, diagonal):
    above = shift_from(source_field, "layer", 1)
    below = shift_from(source_field, "layer", -1)
    north = shift_from(source_field[:, -1:, :], "tx", -1)
    south = shift_from(source_field[:, :1, :], "tx", 1)
    west = shift_from(source_field[:, :, -1:], "ty", -1)
    east = shift_from(source_field[:, :, :1], "ty", 1)
    lateral = (
        jnp.concatenate([source_field[:, 1:, :], south], axis=1)
        + jnp.concatenate([north, source_field[:, :-1, :]], axis=1)
        + jnp.concatenate([source_field[:, :, 1:], east], axis=2)
        + jnp.concatenate([west, source_field[:, :, :-1]], axis=2)
    )
    vertical = above + below
    return diagonal * source_field - lateral - VIA_CONDUCTANCE * vertical


def coarse_sweep(potential, coarse_rhs, coarse_diag, padded):
    beside = (
        padded[..., 2:, 1:-1]
        + padded[..., :-2, 1:-1]
        + padded[..., 1:-1, 2:]
        + padded[..., 1:-1, :-2]
    )
    return (
        potential
        + RELAXATION * (coarse_rhs - (coarse_diag * potential - COARSE_EDGE * beside)) / coarse_diag
    )


def restrict(source_field, gather):
    flat = source_field.reshape(1, -1)
    summed = jnp.dot(
        flat, gather, precision=lax.Precision.HIGHEST, preferred_element_type=jnp.float32
    )
    return summed.reshape(CGX, CGY)


def prolong(potential, gather, shape):
    spread = jnp.dot(
        gather,
        potential.reshape(-1),
        precision=lax.Precision.HIGHEST,
        preferred_element_type=jnp.float32,
    )
    return spread.reshape(shape)


def precondition(residual, diagonal, gather, diag_ext, inside_ext, coarse_diag=None):
    coarse_rhs = restrict(residual, gather)
    if diag_ext is None:
        both = coarse_ext(jnp.stack([coarse_rhs, coarse_diag]))
        coarse_rhs = both[0]
        diag_ext = jnp.where(inside_ext, both[1], 1.0)
    else:
        coarse_rhs = coarse_ext(coarse_rhs)
    whole_diag = diag_ext
    potential = jnp.where(inside_ext, RELAXATION * coarse_rhs / diag_ext, 0.0)
    for sweep_turn in range(SWEEPS - 1):
        potential = coarse_sweep(
            potential[1:-1, 1:-1], coarse_rhs[1:-1, 1:-1], diag_ext[1:-1, 1:-1], potential
        )
        coarse_rhs = coarse_rhs[1:-1, 1:-1]
        diag_ext = diag_ext[1:-1, 1:-1]
        inside_ext = inside_ext[1:-1, 1:-1]
        potential = jnp.where(inside_ext, potential, 0.0)
    return residual / diagonal + prolong(potential, gather, residual.shape), whole_diag


def body(shunt_conductance, agg_map, slot_current, slot_node, slot_count):
    height = shunt_conductance.shape[1]
    breadth = shunt_conductance.shape[2]
    tile_count = slot_count.shape[3]
    capacity = slot_current.shape[4]
    live_mask = lax.broadcasted_iota(jnp.int32, slot_current.shape, 4) < slot_count[..., None]
    currents = jnp.where(live_mask, slot_current, jnp.zeros_like(slot_current))
    targets = slot_node.astype(jnp.float32)
    packed = jnp.stack(
        [currents.reshape(tile_count, capacity), targets.reshape(tile_count, capacity)], axis=1
    )
    arrived = lax.all_to_all(packed, ("tx", "ty"), split_axis=0, concat_axis=0, tiled=True)
    arrived_current = arrived[:, 0, :].reshape(-1)
    node_ids = arrived[:, 1, :].reshape(-1).astype(jnp.int32)
    row_hit = (
        (node_ids // breadth)[:, None] == lax.broadcasted_iota(jnp.int32, (1, height), 1)
    )
    col_hit = (
        (node_ids % breadth)[:, None] == lax.broadcasted_iota(jnp.int32, (1, breadth), 1)
    ).astype(jnp.float32)
    weighted_rows = jnp.where(row_hit, arrived_current[:, None], 0.0)
    sources = lax.dot_general(
        weighted_rows,
        col_hit,
        (((0,), (0,)), ((), ())),
        precision=lax.Precision.HIGHEST,
        preferred_element_type=jnp.float32,
    ).reshape(1, height, breadth)

    gather = (
        agg_map.reshape(-1)[:, None] == lax.broadcasted_iota(jnp.int32, (1, CGX * CGY), 1)
    ).astype(jnp.float32)
    diagonal = shunt_conductance + (4.0 + 2.0 * VIA_CONDUCTANCE)
    coarse_diag = 4.0 * COARSE_EDGE + restrict(shunt_conductance + 2.0 * VIA_CONDUCTANCE, gather)
    row_of = lax.axis_index("tx") * CGX - 2 + lax.broadcasted_iota(jnp.int32, (CGX + 4, CGY + 4), 0)
    col_of = lax.axis_index("ty") * CGY - 2 + lax.broadcasted_iota(jnp.int32, (CGX + 4, CGY + 4), 1)
    inside_ext = (
        (row_of >= 0)
        & (row_of < lax.axis_size("tx") * CGX)
        & (col_of >= 0)
        & (col_of < lax.axis_size("ty") * CGY)
    )

    first, diag_ext = precondition(sources, diagonal, gather, None, inside_ext, coarse_diag)
    basis = [first]
    images = []
    for iteration in range(ITERS):
        images.append(operate(basis[-1], diagonal))
        if iteration + 1 < ITERS:
            smoothed, diag_ext = precondition(images[-1], diagonal, gather, diag_ext, inside_ext)
            basis.append(smoothed - KRYLOV_SHIFT * basis[-1])
    residual_side = [sources] + images[: ITERS - 1]
    left = jnp.stack([field.reshape(-1) for field in residual_side + basis])
    right = jnp.stack([field.reshape(-1) for field in basis + images])
    local = lax.dot_general(
        left,
        right,
        (((1,), (1,)), ((), ())),
        precision=lax.Precision.HIGHEST,
        preferred_element_type=jnp.float32,
    )
    flat = jnp.concatenate([local[:ITERS, :ITERS].reshape(-1), local[ITERS:, ITERS:].reshape(-1)])
    lanes = lax.optimization_barrier(
        jnp.broadcast_to(total(flat)[:, None], (flat.shape[0], LANES))
    ).reshape(-1)

    def entry(index):
        return lanes[index * LANES : (index + 1) * LANES]

    gram_rz = [[entry(i * ITERS + j) for j in range(ITERS)] for i in range(ITERS)]
    gram_za = [[entry((ITERS + i) * ITERS + j) for j in range(ITERS)] for i in range(ITERS)]

    def form(coords_left, gram, coords_right):
        terms = [
            coords_left[i] * gram[i][j] * coords_right[j]
            for i in range(ITERS)
            for j in range(ITERS)
            if coords_left[i] is not None and coords_right[j] is not None
        ]
        result = terms[0]
        for term in terms[1:]:
            result = result + term
        return result

    def scaled_add(first_term, factor, second_term):
        if second_term is None:
            return first_term
        if first_term is None:
            return factor * second_term
        return first_term + factor * second_term

    def smoothed_coords(coords):
        return [
            scaled_add(coords[i], KRYLOV_SHIFT, coords[i + 1]) for i in range(ITERS)
        ]

    residual_coords = [1.0] + [None] * ITERS
    voltage_coords = [None] * ITERS
    direction = [1.0] + [None] * (ITERS - 1)
    curv_now = form(residual_coords, gram_rz, smoothed_coords(residual_coords))
    for iteration in range(ITERS):
        energy = form(direction, gram_za, direction)
        step_size = curv_now / energy
        voltage_coords = [
            scaled_add(voltage_coords[i], step_size, direction[i]) for i in range(ITERS)
        ]
        residual_coords = [residual_coords[0]] + [
            scaled_add(residual_coords[i + 1], -step_size, direction[i]) for i in range(ITERS)
        ]
        if iteration + 1 < ITERS:
            smoothed = smoothed_coords(residual_coords)
            curv_next = form(residual_coords, gram_rz, smoothed)
            ratio = curv_next / curv_now
            direction = [scaled_add(smoothed[i], ratio, direction[i]) for i in range(ITERS)]
            curv_now = curv_next
    voltage = voltage_coords[0][0] * basis[0]
    for index in range(1, ITERS):
        voltage = voltage + voltage_coords[index][0] * basis[index]
    residual = sources
    for index in range(ITERS):
        residual = residual + residual_coords[index + 1][0] * images[index]
    return (voltage, residual)


def solution(mesh):
    in_specs = (
        P("layer", "tx", "ty"),
        P("layer", "tx", "ty"),
        P("layer", "tx", "ty", None, None),
        P("layer", "tx", "ty", None, None),
        P("layer", "tx", "ty", None),
    )
    out_specs = (P("layer", "tx", "ty"), P("layer", "tx", "ty"))
    return jax.shard_map(body, mesh=mesh, in_specs=in_specs, out_specs=out_specs, check_vma=False)
```

```python
import jax
import jax.numpy as jnp
from jax import lax
from jax.sharding import PartitionSpec as P

CGX = 8
CGY = 16
ITERS = 3
SWEEPS = 3


VIA_CONDUCTANCE = 0.5
COARSE_EDGE = 8.0
RELAXATION = 0.6
KRYLOV_SHIFT = 1.0
LANES = 128


def total(vector):
    for axis in ("ty", "tx", "layer"):
        vector = lax.psum(vector, axis)
    return vector


def shift_from(block, axis, offset):
    count = lax.axis_size(axis)
    pairs = [((i + offset) % count, i) for i in range(count)]
    moved = lax.ppermute(block, axis, pairs)
    source = lax.axis_index(axis) + offset
    return jnp.where((source >= 0) & (source < count), moved, jnp.zeros_like(moved))


def shift_from_2d(block, offset_x, offset_y):
    count_x = lax.axis_size("tx")
    count_y = lax.axis_size("ty")
    pairs = []
    for i in range(count_x):
        for j in range(count_y):
            si, sj = i + offset_x, j + offset_y
            if 0 <= si < count_x and 0 <= sj < count_y:
                pairs.append((si * count_y + sj, i * count_y + j))
    return lax.ppermute(block, ("tx", "ty"), pairs)


def coarse_ext(field):
    north = shift_from(field[..., -2:, :], "tx", -1)
    south = shift_from(field[..., :2, :], "tx", 1)
    rows = jnp.concatenate([north, field, south], axis=-2)
    west = shift_from(rows[..., :, -2:], "ty", -1)
    east = shift_from(rows[..., :, :2], "ty", 1)
    return jnp.concatenate([west, rows, east], axis=-1)


def operate(source_field, diagonal):
    above = shift_from(source_field, "layer", 1)
    below = shift_from(source_field, "layer", -1)
    north = shift_from(source_field[:, -1:, :], "tx", -1)
    south = shift_from(source_field[:, :1, :], "tx", 1)
    west = shift_from(source_field[:, :, -1:], "ty", -1)
    east = shift_from(source_field[:, :, :1], "ty", 1)
    lateral = (
        jnp.concatenate([source_field[:, 1:, :], south], axis=1)
        + jnp.concatenate([north, source_field[:, :-1, :]], axis=1)
        + jnp.concatenate([source_field[:, :, 1:], east], axis=2)
        + jnp.concatenate([west, source_field[:, :, :-1]], axis=2)
    )
    vertical = above + below
    return diagonal * source_field - lateral - VIA_CONDUCTANCE * vertical


def coarse_sweep(potential, coarse_rhs, coarse_diag, padded):
    beside = (
        padded[..., 2:, 1:-1]
        + padded[..., :-2, 1:-1]
        + padded[..., 1:-1, 2:]
        + padded[..., 1:-1, :-2]
    )
    return (
        potential
        + RELAXATION * (coarse_rhs - (coarse_diag * potential - COARSE_EDGE * beside)) / coarse_diag
    )


def restrict(source_field, gather):
    flat = source_field.reshape(1, -1)
    summed = jnp.dot(
        flat, gather, precision=lax.Precision.HIGH, preferred_element_type=jnp.float32
    )
    return summed.reshape(CGX, CGY)


def prolong(potential, gather, shape):
    spread = jnp.dot(
        gather,
        potential.reshape(-1),
        precision=lax.Precision.HIGH,
        preferred_element_type=jnp.float32,
    )
    return spread.reshape(shape)


def precondition(residual, diagonal, gather, diag_ext, inside_ext, coarse_diag=None):
    coarse_rhs = restrict(residual, gather)
    if diag_ext is None:
        both = coarse_ext(jnp.stack([coarse_rhs, coarse_diag]))
        coarse_rhs = both[0]
        diag_ext = jnp.where(inside_ext, both[1], 1.0)
    else:
        coarse_rhs = coarse_ext(coarse_rhs)
    whole_diag = diag_ext
    potential = jnp.where(inside_ext, RELAXATION * coarse_rhs / diag_ext, 0.0)
    for sweep_turn in range(SWEEPS - 1):
        potential = coarse_sweep(
            potential[1:-1, 1:-1], coarse_rhs[1:-1, 1:-1], diag_ext[1:-1, 1:-1], potential
        )
        coarse_rhs = coarse_rhs[1:-1, 1:-1]
        diag_ext = diag_ext[1:-1, 1:-1]
        inside_ext = inside_ext[1:-1, 1:-1]
        potential = jnp.where(inside_ext, potential, 0.0)
    return residual / diagonal + prolong(potential, gather, residual.shape), whole_diag


def body(shunt_conductance, agg_map, slot_current, slot_node, slot_count):
    height = shunt_conductance.shape[1]
    breadth = shunt_conductance.shape[2]
    tile_count = slot_count.shape[3]
    capacity = slot_current.shape[4]
    live_mask = lax.broadcasted_iota(jnp.int32, slot_current.shape, 4) < slot_count[..., None]
    currents = jnp.where(live_mask, slot_current, jnp.zeros_like(slot_current))
    targets = slot_node.astype(jnp.float32)
    packed = jnp.stack(
        [currents.reshape(tile_count, capacity), targets.reshape(tile_count, capacity)], axis=1
    )
    arrived = lax.all_to_all(packed, ("tx", "ty"), split_axis=0, concat_axis=0, tiled=True)
    arrived_current = arrived[:, 0, :].reshape(-1)
    node_ids = arrived[:, 1, :].reshape(-1).astype(jnp.int32)
    row_hit = (
        (node_ids // breadth)[:, None] == lax.broadcasted_iota(jnp.int32, (1, height), 1)
    )
    col_hit = (
        (node_ids % breadth)[:, None] == lax.broadcasted_iota(jnp.int32, (1, breadth), 1)
    ).astype(jnp.float32)
    weighted_rows = jnp.where(row_hit, arrived_current[:, None], 0.0)
    sources = lax.dot_general(
        weighted_rows,
        col_hit,
        (((0,), (0,)), ((), ())),
        precision=lax.Precision.HIGH,
        preferred_element_type=jnp.float32,
    ).reshape(1, height, breadth)

    gather = (
        agg_map.reshape(-1)[:, None] == lax.broadcasted_iota(jnp.int32, (1, CGX * CGY), 1)
    ).astype(jnp.float32)
    diagonal = shunt_conductance + (4.0 + 2.0 * VIA_CONDUCTANCE)
    coarse_diag = 4.0 * COARSE_EDGE + restrict(shunt_conductance + 2.0 * VIA_CONDUCTANCE, gather)
    row_of = lax.axis_index("tx") * CGX - 2 + lax.broadcasted_iota(jnp.int32, (CGX + 4, CGY + 4), 0)
    col_of = lax.axis_index("ty") * CGY - 2 + lax.broadcasted_iota(jnp.int32, (CGX + 4, CGY + 4), 1)
    inside_ext = (
        (row_of >= 0)
        & (row_of < lax.axis_size("tx") * CGX)
        & (col_of >= 0)
        & (col_of < lax.axis_size("ty") * CGY)
    )

    first, diag_ext = precondition(sources, diagonal, gather, None, inside_ext, coarse_diag)
    basis = [first]
    images = []
    for iteration in range(ITERS):
        images.append(operate(basis[-1], diagonal))
        if iteration + 1 < ITERS:
            smoothed, diag_ext = precondition(images[-1], diagonal, gather, diag_ext, inside_ext)
            basis.append(smoothed - KRYLOV_SHIFT * basis[-1])
    residual_side = [sources] + images[: ITERS - 1]
    left = jnp.stack([field.reshape(-1) for field in residual_side + basis])
    right = jnp.stack([field.reshape(-1) for field in basis + images])
    local = lax.dot_general(
        left,
        right,
        (((1,), (1,)), ((), ())),
        precision=lax.Precision.HIGHEST,
        preferred_element_type=jnp.float32,
    )
    flat = jnp.concatenate([local[:ITERS, :ITERS].reshape(-1), local[ITERS:, ITERS:].reshape(-1)])
    lanes = lax.optimization_barrier(
        jnp.broadcast_to(total(flat)[:, None], (flat.shape[0], LANES))
    ).reshape(-1)

    def entry(index):
        return lanes[index * LANES : (index + 1) * LANES]

    gram_rz = [[entry(i * ITERS + j) for j in range(ITERS)] for i in range(ITERS)]
    gram_za = [[entry((ITERS + i) * ITERS + j) for j in range(ITERS)] for i in range(ITERS)]

    def form(coords_left, gram, coords_right):
        terms = [
            coords_left[i] * gram[i][j] * coords_right[j]
            for i in range(ITERS)
            for j in range(ITERS)
            if coords_left[i] is not None and coords_right[j] is not None
        ]
        result = terms[0]
        for term in terms[1:]:
            result = result + term
        return result

    def scaled_add(first_term, factor, second_term):
        if second_term is None:
            return first_term
        if first_term is None:
            return factor * second_term
        return first_term + factor * second_term

    def smoothed_coords(coords):
        return [
            scaled_add(coords[i], KRYLOV_SHIFT, coords[i + 1]) for i in range(ITERS)
        ]

    residual_coords = [1.0] + [None] * ITERS
    voltage_coords = [None] * ITERS
    direction = [1.0] + [None] * (ITERS - 1)
    curv_now = form(residual_coords, gram_rz, smoothed_coords(residual_coords))
    for iteration in range(ITERS):
        energy = form(direction, gram_za, direction)
        step_size = curv_now / energy
        voltage_coords = [
            scaled_add(voltage_coords[i], step_size, direction[i]) for i in range(ITERS)
        ]
        residual_coords = [residual_coords[0]] + [
            scaled_add(residual_coords[i + 1], -step_size, direction[i]) for i in range(ITERS)
        ]
        if iteration + 1 < ITERS:
            smoothed = smoothed_coords(residual_coords)
            curv_next = form(residual_coords, gram_rz, smoothed)
            ratio = curv_next / curv_now
            direction = [scaled_add(smoothed[i], ratio, direction[i]) for i in range(ITERS)]
            curv_now = curv_next
    voltage = voltage_coords[0][0] * basis[0]
    for index in range(1, ITERS):
        voltage = voltage + voltage_coords[index][0] * basis[index]
    residual = sources
    for index in range(ITERS):
        residual = residual + residual_coords[index + 1][0] * images[index]
    return (voltage, residual)


def solution(mesh):
    in_specs = (
        P("layer", "tx", "ty"),
        P("layer", "tx", "ty"),
        P("layer", "tx", "ty", None, None),
        P("layer", "tx", "ty", None, None),
        P("layer", "tx", "ty", None),
    )
    out_specs = (P("layer", "tx", "ty"), P("layer", "tx", "ty"))
    return jax.shard_map(body, mesh=mesh, in_specs=in_specs, out_specs=out_specs, check_vma=False)
```

```python
import jax
import jax.numpy as jnp
from jax import lax
from jax.sharding import PartitionSpec as P

CGX = 8
CGY = 16
ITERS = 3
SWEEPS = 3


VIA_CONDUCTANCE = 0.5
COARSE_EDGE = 8.0
RELAXATION = 0.6
KRYLOV_SHIFT = 1.0
LANES = 128


def total(vector):
    for axis in ("ty", "tx", "layer"):
        vector = lax.psum(vector, axis)
    return vector


def shift_from(block, axis, offset):
    count = lax.axis_size(axis)
    pairs = [((i + offset) % count, i) for i in range(count)]
    moved = lax.ppermute(block, axis, pairs)
    source = lax.axis_index(axis) + offset
    return jnp.where((source >= 0) & (source < count), moved, jnp.zeros_like(moved))


def shift_from_2d(block, offset_x, offset_y):
    count_x = lax.axis_size("tx")
    count_y = lax.axis_size("ty")
    pairs = []
    for i in range(count_x):
        for j in range(count_y):
            si, sj = i + offset_x, j + offset_y
            if 0 <= si < count_x and 0 <= sj < count_y:
                pairs.append((si * count_y + sj, i * count_y + j))
    return lax.ppermute(block, ("tx", "ty"), pairs)


def coarse_ext(field):
    north = shift_from(field[..., -2:, :], "tx", -1)
    south = shift_from(field[..., :2, :], "tx", 1)
    rows = jnp.concatenate([north, field, south], axis=-2)
    west = shift_from(rows[..., :, -2:], "ty", -1)
    east = shift_from(rows[..., :, :2], "ty", 1)
    return jnp.concatenate([west, rows, east], axis=-1)


def operate(source_field, diagonal):
    above = shift_from(source_field, "layer", 1)
    below = shift_from(source_field, "layer", -1)
    north = shift_from(source_field[:, -1:, :], "tx", -1)
    south = shift_from(source_field[:, :1, :], "tx", 1)
    west = shift_from(source_field[:, :, -1:], "ty", -1)
    east = shift_from(source_field[:, :, :1], "ty", 1)
    lateral = (
        jnp.concatenate([source_field[:, 1:, :], south], axis=1)
        + jnp.concatenate([north, source_field[:, :-1, :]], axis=1)
        + jnp.concatenate([source_field[:, :, 1:], east], axis=2)
        + jnp.concatenate([west, source_field[:, :, :-1]], axis=2)
    )
    vertical = above + below
    return diagonal * source_field - lateral - VIA_CONDUCTANCE * vertical


def coarse_sweep(potential, coarse_rhs, coarse_diag, padded):
    beside = (
        padded[..., 2:, 1:-1]
        + padded[..., :-2, 1:-1]
        + padded[..., 1:-1, 2:]
        + padded[..., 1:-1, :-2]
    )
    return (
        potential
        + RELAXATION * (coarse_rhs - (coarse_diag * potential - COARSE_EDGE * beside)) / coarse_diag
    )


def restrict(source_field, gather):
    flat = source_field.reshape(1, -1)
    summed = jnp.dot(
        flat, gather, precision=lax.Precision.HIGH, preferred_element_type=jnp.float32
    )
    return summed.reshape(CGX, CGY)


def prolong(potential, gather, shape):
    spread = jnp.dot(
        gather,
        potential.reshape(-1),
        precision=lax.Precision.HIGH,
        preferred_element_type=jnp.float32,
    )
    return spread.reshape(shape)


def precondition(residual, diagonal, gather, diag_ext, inside_ext, coarse_diag=None):
    coarse_rhs = restrict(residual, gather)
    if diag_ext is None:
        both = coarse_ext(jnp.stack([coarse_rhs, coarse_diag]))
        coarse_rhs = both[0]
        diag_ext = jnp.where(inside_ext, both[1], 1.0)
    else:
        coarse_rhs = coarse_ext(coarse_rhs)
    whole_diag = diag_ext
    potential = jnp.where(inside_ext, RELAXATION * coarse_rhs / diag_ext, 0.0)
    for sweep_turn in range(SWEEPS - 1):
        potential = coarse_sweep(
            potential[1:-1, 1:-1], coarse_rhs[1:-1, 1:-1], diag_ext[1:-1, 1:-1], potential
        )
        coarse_rhs = coarse_rhs[1:-1, 1:-1]
        diag_ext = diag_ext[1:-1, 1:-1]
        inside_ext = inside_ext[1:-1, 1:-1]
        potential = jnp.where(inside_ext, potential, 0.0)
    return residual / diagonal + prolong(potential, gather, residual.shape), whole_diag


def body(shunt_conductance, agg_map, slot_current, slot_node, slot_count):
    height = shunt_conductance.shape[1]
    breadth = shunt_conductance.shape[2]
    tile_count = slot_count.shape[3]
    capacity = slot_current.shape[4]
    row = lax.broadcasted_iota(jnp.int32, (tile_count, 2, capacity), 1)
    slot = lax.broadcasted_iota(jnp.int32, (tile_count, 2, capacity), 2)
    live_mask = slot < slot_count.reshape(tile_count, 1, 1)
    currents = jnp.where(live_mask, slot_current.reshape(tile_count, 1, capacity), 0.0)
    packed = jnp.where(
        row == 0, currents, slot_node.reshape(tile_count, 1, capacity).astype(jnp.float32)
    )
    arrived = lax.all_to_all(packed, ("tx", "ty"), split_axis=0, concat_axis=0, tiled=True)
    arrived_current = arrived[:, 0, :].reshape(-1)
    node_ids = arrived[:, 1, :].reshape(-1).astype(jnp.int32)
    row_hit = (
        (node_ids // breadth)[:, None] == lax.broadcasted_iota(jnp.int32, (1, height), 1)
    )
    col_hit = (
        (node_ids % breadth)[:, None] == lax.broadcasted_iota(jnp.int32, (1, breadth), 1)
    ).astype(jnp.float32)
    weighted_rows = jnp.where(row_hit, arrived_current[:, None], 0.0)
    sources = lax.dot_general(
        weighted_rows,
        col_hit,
        (((0,), (0,)), ((), ())),
        precision=lax.Precision.HIGH,
        preferred_element_type=jnp.float32,
    ).reshape(1, height, breadth)

    gather = (
        agg_map.reshape(-1)[:, None] == lax.broadcasted_iota(jnp.int32, (1, CGX * CGY), 1)
    ).astype(jnp.float32)
    diagonal = shunt_conductance + (4.0 + 2.0 * VIA_CONDUCTANCE)
    coarse_diag = 4.0 * COARSE_EDGE + restrict(shunt_conductance + 2.0 * VIA_CONDUCTANCE, gather)
    row_of = lax.axis_index("tx") * CGX - 2 + lax.broadcasted_iota(jnp.int32, (CGX + 4, CGY + 4), 0)
    col_of = lax.axis_index("ty") * CGY - 2 + lax.broadcasted_iota(jnp.int32, (CGX + 4, CGY + 4), 1)
    inside_ext = (
        (row_of >= 0)
        & (row_of < lax.axis_size("tx") * CGX)
        & (col_of >= 0)
        & (col_of < lax.axis_size("ty") * CGY)
    )

    first, diag_ext = precondition(sources, diagonal, gather, None, inside_ext, coarse_diag)
    basis = [first]
    images = []
    for iteration in range(ITERS):
        images.append(operate(basis[-1], diagonal))
        if iteration + 1 < ITERS:
            smoothed, diag_ext = precondition(images[-1], diagonal, gather, diag_ext, inside_ext)
            basis.append(smoothed - KRYLOV_SHIFT * basis[-1])
    residual_side = [sources] + images[: ITERS - 1]
    left = jnp.stack([field.reshape(-1) for field in residual_side + basis])
    right = jnp.stack([field.reshape(-1) for field in basis + images])
    local = lax.dot_general(
        left,
        right,
        (((1,), (1,)), ((), ())),
        precision=lax.Precision.HIGHEST,
        preferred_element_type=jnp.float32,
    )
    flat = jnp.concatenate([local[:ITERS, :ITERS].reshape(-1), local[ITERS:, ITERS:].reshape(-1)])
    lanes = lax.optimization_barrier(
        jnp.broadcast_to(total(flat)[:, None], (flat.shape[0], LANES))
    ).reshape(-1)

    def entry(index):
        return lanes[index * LANES : (index + 1) * LANES]

    gram_rz = [[entry(i * ITERS + j) for j in range(ITERS)] for i in range(ITERS)]
    gram_za = [[entry((ITERS + i) * ITERS + j) for j in range(ITERS)] for i in range(ITERS)]

    def form(coords_left, gram, coords_right):
        terms = [
            coords_left[i] * gram[i][j] * coords_right[j]
            for i in range(ITERS)
            for j in range(ITERS)
            if coords_left[i] is not None and coords_right[j] is not None
        ]
        result = terms[0]
        for term in terms[1:]:
            result = result + term
        return result

    def scaled_add(first_term, factor, second_term):
        if second_term is None:
            return first_term
        if first_term is None:
            return factor * second_term
        return first_term + factor * second_term

    def smoothed_coords(coords):
        return [
            scaled_add(coords[i], KRYLOV_SHIFT, coords[i + 1]) for i in range(ITERS)
        ]

    residual_coords = [1.0] + [None] * ITERS
    voltage_coords = [None] * ITERS
    direction = [1.0] + [None] * (ITERS - 1)
    curv_now = form(residual_coords, gram_rz, smoothed_coords(residual_coords))
    for iteration in range(ITERS):
        energy = form(direction, gram_za, direction)
        step_size = curv_now / energy
        voltage_coords = [
            scaled_add(voltage_coords[i], step_size, direction[i]) for i in range(ITERS)
        ]
        residual_coords = [residual_coords[0]] + [
            scaled_add(residual_coords[i + 1], -step_size, direction[i]) for i in range(ITERS)
        ]
        if iteration + 1 < ITERS:
            smoothed = smoothed_coords(residual_coords)
            curv_next = form(residual_coords, gram_rz, smoothed)
            ratio = curv_next / curv_now
            direction = [scaled_add(smoothed[i], ratio, direction[i]) for i in range(ITERS)]
            curv_now = curv_next
    voltage = voltage_coords[0][0] * basis[0]
    for index in range(1, ITERS):
        voltage = voltage + voltage_coords[index][0] * basis[index]
    residual = sources
    for index in range(ITERS):
        residual = residual + residual_coords[index + 1][0] * images[index]
    return (voltage, residual)


def solution(mesh):
    in_specs = (
        P("layer", "tx", "ty"),
        P("layer", "tx", "ty"),
        P("layer", "tx", "ty", None, None),
        P("layer", "tx", "ty", None, None),
        P("layer", "tx", "ty", None),
    )
    out_specs = (P("layer", "tx", "ty"), P("layer", "tx", "ty"))
    return jax.shard_map(body, mesh=mesh, in_specs=in_specs, out_specs=out_specs, check_vma=False)
```

```python
import jax
import jax.numpy as jnp
from jax import lax
from jax.sharding import PartitionSpec as P

CGX = 8
CGY = 16
ITERS = 3
SWEEPS = 3


VIA_CONDUCTANCE = 0.5
COARSE_EDGE = 8.0
RELAXATION = 0.6
KRYLOV_SHIFT = 1.0
LANES = 128


def total(vector):
    for axis in ("ty", "tx", "layer"):
        vector = lax.psum(vector, axis)
    return vector


def shift_from(block, axis, offset):
    count = lax.axis_size(axis)
    pairs = [((i + offset) % count, i) for i in range(count)]
    moved = lax.ppermute(block, axis, pairs)
    source = lax.axis_index(axis) + offset
    return jnp.where((source >= 0) & (source < count), moved, jnp.zeros_like(moved))


def shift_from_2d(block, offset_x, offset_y):
    count_x = lax.axis_size("tx")
    count_y = lax.axis_size("ty")
    pairs = []
    for i in range(count_x):
        for j in range(count_y):
            si, sj = i + offset_x, j + offset_y
            if 0 <= si < count_x and 0 <= sj < count_y:
                pairs.append((si * count_y + sj, i * count_y + j))
    return lax.ppermute(block, ("tx", "ty"), pairs)


def coarse_ext(field):
    north = shift_from(field[..., -2:, :], "tx", -1)
    south = shift_from(field[..., :2, :], "tx", 1)
    rows = jnp.concatenate([north, field, south], axis=-2)
    west = shift_from(rows[..., :, -2:], "ty", -1)
    east = shift_from(rows[..., :, :2], "ty", 1)
    return jnp.concatenate([west, rows, east], axis=-1)


def operate(source_field, diagonal):
    above = shift_from(source_field, "layer", 1)
    below = shift_from(source_field, "layer", -1)
    north = shift_from(source_field[:, -1:, :], "tx", -1)
    south = shift_from(source_field[:, :1, :], "tx", 1)
    rim_shape = (source_field.shape[0], source_field.shape[1], 1)
    west = shift_from(source_field[:, :, -1].reshape(1, -1), "ty", -1).reshape(rim_shape)
    east = shift_from(source_field[:, :, 0].reshape(1, -1), "ty", 1).reshape(rim_shape)
    lateral = (
        jnp.concatenate([source_field[:, 1:, :], south], axis=1)
        + jnp.concatenate([north, source_field[:, :-1, :]], axis=1)
        + jnp.concatenate([source_field[:, :, 1:], east], axis=2)
        + jnp.concatenate([west, source_field[:, :, :-1]], axis=2)
    )
    vertical = above + below
    return diagonal * source_field - lateral - VIA_CONDUCTANCE * vertical


def coarse_sweep(potential, coarse_rhs, coarse_diag, padded):
    beside = (
        padded[..., 2:, 1:-1]
        + padded[..., :-2, 1:-1]
        + padded[..., 1:-1, 2:]
        + padded[..., 1:-1, :-2]
    )
    return (
        potential
        + RELAXATION * (coarse_rhs - (coarse_diag * potential - COARSE_EDGE * beside)) / coarse_diag
    )


def restrict(source_field, gather):
    flat = source_field.reshape(1, -1)
    summed = jnp.dot(
        flat, gather, precision=lax.Precision.HIGH, preferred_element_type=jnp.float32
    )
    return summed.reshape(CGX, CGY)


def prolong(potential, gather, shape):
    spread = jnp.dot(
        gather,
        potential.reshape(-1),
        precision=lax.Precision.HIGH,
        preferred_element_type=jnp.float32,
    )
    return spread.reshape(shape)


def precondition(residual, diagonal, gather, diag_ext, inside_ext, coarse_diag=None):
    coarse_rhs = restrict(residual, gather)
    if diag_ext is None:
        both = coarse_ext(jnp.stack([coarse_rhs, coarse_diag]))
        coarse_rhs = both[0]
        diag_ext = jnp.where(inside_ext, both[1], 1.0)
    else:
        coarse_rhs = coarse_ext(coarse_rhs)
    whole_diag = diag_ext
    potential = jnp.where(inside_ext, RELAXATION * coarse_rhs / diag_ext, 0.0)
    for sweep_turn in range(SWEEPS - 1):
        potential = coarse_sweep(
            potential[1:-1, 1:-1], coarse_rhs[1:-1, 1:-1], diag_ext[1:-1, 1:-1], potential
        )
        coarse_rhs = coarse_rhs[1:-1, 1:-1]
        diag_ext = diag_ext[1:-1, 1:-1]
        inside_ext = inside_ext[1:-1, 1:-1]
        potential = jnp.where(inside_ext, potential, 0.0)
    return residual / diagonal + prolong(potential, gather, residual.shape), whole_diag


def body(shunt_conductance, agg_map, slot_current, slot_node, slot_count):
    height = shunt_conductance.shape[1]
    breadth = shunt_conductance.shape[2]
    tile_count = slot_count.shape[3]
    capacity = slot_current.shape[4]
    live_mask = lax.broadcasted_iota(jnp.int32, slot_current.shape, 4) < slot_count[..., None]
    currents = jnp.where(live_mask, slot_current, jnp.zeros_like(slot_current))
    targets = slot_node.astype(jnp.float32)
    packed = jnp.stack(
        [currents.reshape(tile_count, capacity), targets.reshape(tile_count, capacity)], axis=1
    )
    arrived = lax.all_to_all(packed, ("tx", "ty"), split_axis=0, concat_axis=0, tiled=True)
    arrived_current = arrived[:, 0, :].reshape(-1)
    node_ids = arrived[:, 1, :].reshape(-1).astype(jnp.int32)
    row_hit = (
        (node_ids // breadth)[:, None] == lax.broadcasted_iota(jnp.int32, (1, height), 1)
    )
    col_hit = (
        (node_ids % breadth)[:, None] == lax.broadcasted_iota(jnp.int32, (1, breadth), 1)
    ).astype(jnp.float32)
    weighted_rows = jnp.where(row_hit, arrived_current[:, None], 0.0)
    sources = lax.dot_general(
        weighted_rows,
        col_hit,
        (((0,), (0,)), ((), ())),
        precision=lax.Precision.HIGH,
        preferred_element_type=jnp.float32,
    ).reshape(1, height, breadth)

    gather = (
        agg_map.reshape(-1)[:, None] == lax.broadcasted_iota(jnp.int32, (1, CGX * CGY), 1)
    ).astype(jnp.float32)
    diagonal = shunt_conductance + (4.0 + 2.0 * VIA_CONDUCTANCE)
    coarse_diag = 4.0 * COARSE_EDGE + restrict(shunt_conductance + 2.0 * VIA_CONDUCTANCE, gather)
    row_of = lax.axis_index("tx") * CGX - 2 + lax.broadcasted_iota(jnp.int32, (CGX + 4, CGY + 4), 0)
    col_of = lax.axis_index("ty") * CGY - 2 + lax.broadcasted_iota(jnp.int32, (CGX + 4, CGY + 4), 1)
    inside_ext = (
        (row_of >= 0)
        & (row_of < lax.axis_size("tx") * CGX)
        & (col_of >= 0)
        & (col_of < lax.axis_size("ty") * CGY)
    )

    first, diag_ext = precondition(sources, diagonal, gather, None, inside_ext, coarse_diag)
    basis = [first]
    images = []
    for iteration in range(ITERS):
        images.append(operate(basis[-1], diagonal))
        if iteration + 1 < ITERS:
            smoothed, diag_ext = precondition(images[-1], diagonal, gather, diag_ext, inside_ext)
            basis.append(smoothed - KRYLOV_SHIFT * basis[-1])
    residual_side = [sources] + images[: ITERS - 1]
    left = jnp.stack([field.reshape(-1) for field in residual_side + basis])
    right = jnp.stack([field.reshape(-1) for field in basis + images])
    local = lax.dot_general(
        left,
        right,
        (((1,), (1,)), ((), ())),
        precision=lax.Precision.HIGHEST,
        preferred_element_type=jnp.float32,
    )
    flat = jnp.concatenate([local[:ITERS, :ITERS].reshape(-1), local[ITERS:, ITERS:].reshape(-1)])
    lanes = lax.optimization_barrier(
        jnp.broadcast_to(total(flat)[:, None], (flat.shape[0], LANES))
    ).reshape(-1)

    def entry(index):
        return lanes[index * LANES : (index + 1) * LANES]

    gram_rz = [[entry(i * ITERS + j) for j in range(ITERS)] for i in range(ITERS)]
    gram_za = [[entry((ITERS + i) * ITERS + j) for j in range(ITERS)] for i in range(ITERS)]

    def form(coords_left, gram, coords_right):
        terms = [
            coords_left[i] * gram[i][j] * coords_right[j]
            for i in range(ITERS)
            for j in range(ITERS)
            if coords_left[i] is not None and coords_right[j] is not None
        ]
        result = terms[0]
        for term in terms[1:]:
            result = result + term
        return result

    def scaled_add(first_term, factor, second_term):
        if second_term is None:
            return first_term
        if first_term is None:
            return factor * second_term
        return first_term + factor * second_term

    def smoothed_coords(coords):
        return [
            scaled_add(coords[i], KRYLOV_SHIFT, coords[i + 1]) for i in range(ITERS)
        ]

    residual_coords = [1.0] + [None] * ITERS
    voltage_coords = [None] * ITERS
    direction = [1.0] + [None] * (ITERS - 1)
    curv_now = form(residual_coords, gram_rz, smoothed_coords(residual_coords))
    for iteration in range(ITERS):
        energy = form(direction, gram_za, direction)
        step_size = curv_now / energy
        voltage_coords = [
            scaled_add(voltage_coords[i], step_size, direction[i]) for i in range(ITERS)
        ]
        residual_coords = [residual_coords[0]] + [
            scaled_add(residual_coords[i + 1], -step_size, direction[i]) for i in range(ITERS)
        ]
        if iteration + 1 < ITERS:
            smoothed = smoothed_coords(residual_coords)
            curv_next = form(residual_coords, gram_rz, smoothed)
            ratio = curv_next / curv_now
            direction = [scaled_add(smoothed[i], ratio, direction[i]) for i in range(ITERS)]
            curv_now = curv_next
    voltage = voltage_coords[0][0] * basis[0]
    for index in range(1, ITERS):
        voltage = voltage + voltage_coords[index][0] * basis[index]
    residual = sources
    for index in range(ITERS):
        residual = residual + residual_coords[index + 1][0] * images[index]
    return (voltage, residual)


def solution(mesh):
    in_specs = (
        P("layer", "tx", "ty"),
        P("layer", "tx", "ty"),
        P("layer", "tx", "ty", None, None),
        P("layer", "tx", "ty", None, None),
        P("layer", "tx", "ty", None),
    )
    out_specs = (P("layer", "tx", "ty"), P("layer", "tx", "ty"))
    return jax.shard_map(body, mesh=mesh, in_specs=in_specs, out_specs=out_specs, check_vma=False)
```
